32 devices in a mesh: dp: 4 (over z), seq: 2 (over y), expert: 4 (over x, core).
Axes of the slice: x: 2, y: 2, z: 4, core: 2. Of those that a mesh axis runs over, the one named last changes fastest.
Arguments:
- out_grad: bfloat16 [4096, 1024], P(('dp', 'seq', 'expert')), may hold values from -6 to 6
- routes: int32 [4096, 2], P(('dp', 'seq', 'expert')), may hold values from 0 to 3, all different within a row; in each aligned block of 128 rows (0 to 127, 128 to 255, ...) at most 72 rows name the same one
- gates: bfloat16 [4096, 2], P(('dp', 'seq', 'expert')), may hold values from 0.099609375 to 0.8984375
- saved_input: bfloat16 [4, 4, 4, 2, 72, 1024], P('dp', 'expert'), may hold values from -6 to 6
- saved_preact: bfloat16 [4, 4, 4, 2, 72, 2048], P('dp', 'expert', None, None, None, 'seq'), may hold values from -6 to 6
- w_in: bfloat16 [4, 1024, 2048], P('expert', None, 'seq'), may hold values from -0.1875 to 0.1875
- w_out: bfloat16 [4, 2048, 1024], P('expert', 'seq'), may hold values from -0.125 to 0.125
Outputs:
- input_grad: bfloat16 [4096, 1024], P(('dp', 'seq', 'expert'))
- gate_grad: bfloat16 [4096, 2], P(('dp', 'seq', 'expert'))
- weight_grad: float32 [4, 1024, 2048], P('expert', 'dp', 'seq')
The draws below stay inside these ranges and needn't reach their ends.
Inputs may be any that keep to these rules, and one draw needn't show every extreme that they name: `routes`: the two experts of a token differ; within the 128 tokens of one device no expert is chosen more than 72 times, a bound that some block reaches.
All inputs are finite; a program needn't handle non-finite values.
Results may differ from the reference program's by a relative error of at most 0.0058.
Values may be sent and summed in bfloat16 or wider, within the bound.
No kernel may reach another device: no remote copies, remote signals or barrier semaphores. Data moves between devices by JAX's collectives and lax.ppermute only.
A program may use at most 64 MiB of HBM per device.

```python
import math
import jax
import jax.numpy as jnp
import numpy as np
from jax import lax

D = 1024
FF = 2048
TOK_DEV = 128
EXPERTS = 4
MOST = 72
TOKENS = 4096
N_DP = 4
N_SEQ = 2
N_EXPERT = 4


def spiked(result, own_key, source, target, blocks, factor):
    def block_of(axis_at):
        return (jnp.arange(result.shape[axis_at]) // (result.shape[axis_at] // blocks)).reshape((-1,) + (1,) * (result.ndim - 1 - axis_at))

    first = jax.random.permutation(own_key, blocks)[block_of(target)]
    other_side = (block_of(target) + blocks // 2) % blocks
    return jnp.where((block_of(source) == first) | (block_of(source) == other_side), factor * result, result)


def steps_of(rng, dims, split, low, top_value):
    loudness = 1.0
    for position, blocks in split:
        heights = jax.random.uniform(jax.random.fold_in(jax.random.fold_in(rng, 6), position), (blocks,), jnp.float32, low / len(split), top_value / len(split))
        loudness = loudness * jnp.repeat(jnp.exp(heights), dims[position] // blocks).reshape((-1,) + (1,) * (len(dims) - 1 - position))
    return loudness


def shared_out(key, own, number, rows, amount, top, bound, lean):
    ranking = jax.random.permutation(key, amount)
    heavy_load, ordinary = portions_of(amount, rows * top, bound, lean, True), portions_of(amount, rows * top, bound, lean, False)
    places = jnp.arange(amount)

    def named(lengths, turn):
        used = int((lengths > 0).sum())
        fixed = max(1, used // 4)
        passed = fixed + (places - fixed + turn * (used - fixed)) % max(1, amount - fixed)
        return jnp.zeros((amount,), jnp.int32).at[ranking[jnp.where(places < fixed, places, passed)]].set(jnp.asarray(lengths, jnp.int32))

    lengths = jnp.where(number % 4 == 0, named(heavy_load, number // 4), named(ordinary, number - number // 4 - 1))
    mixed = jax.random.permutation(jax.random.fold_in(own, 3), amount)
    giver, taker = mixed[0:amount // 2 * 2:2], mixed[1:amount // 2 * 2:2]
    slack = jnp.minimum(lengths[giver] - 1, bound - lengths[taker]) // 2
    slack = jnp.where((giver == ranking[0]) | (taker == ranking[0]) | (lengths[taker] == 0), 0, jnp.maximum(slack, 0))
    passed = jax.random.randint(jax.random.fold_in(own, 4), (amount // 2,), 0, 1 << 20) % (slack + 1)
    lengths = lengths.at[giver].add(-passed).at[taker].add(passed)
    items = jnp.searchsorted(jnp.cumsum(lengths), jnp.arange(rows * top), side="right").astype(jnp.int32)
    listing = items.reshape(top, rows).T
    listing = listing[jax.random.permutation(jax.random.fold_in(own, 1), rows)]
    turn = jax.random.randint(jax.random.fold_in(own, 2), (rows, 1), 0, top)
    return jnp.take_along_axis(listing, (jnp.arange(top)[None, :] + turn) % top, axis=1)


def portions_of(number_of, total, bound, skew, full):
    weights = [(1 << 20) // math.isqrt(rank ** skew) + 1 for rank in range(1, number_of + 1)]
    largest = bound if full else min(bound, max(-(-total // number_of), total * weights[0] // sum(weights)))
    least = 1 if total - largest >= number_of - 1 else 0
    counts, surplus = [largest] + [least] * (number_of - 1), total - largest - least * (number_of - 1)
    while surplus > 0:
        candidates = [i for i in range(1, number_of) if counts[i] < largest] or [i for i in range(1, number_of) if counts[i] < bound]
        mass, remaining = sum([weights[i] for i in candidates]), surplus
        for i in candidates:
            extra = min(bound - counts[i], max(1, remaining * weights[i] // mass), surplus)
            counts[i] = counts[i] + extra
            surplus = surplus - extra
    return np.array(counts)


def normal_values(stream_key, extent, deviation, most, pieces=(), kind=jnp.bfloat16):
    values = deviation * jax.random.normal(stream_key, extent, jnp.float32)
    if pieces:
        values = values * steps_of(stream_key, extent, pieces, -0.22, 0.18)
    return jnp.clip(values, -most, most).astype(kind)


def gaussian_with(stream_key, shape, scale, bound, pieces, heavy, kind=jnp.bfloat16):
    result = scale * jax.random.normal(stream_key, shape, jnp.float32)
    if pieces:
        result = result * steps_of(stream_key, shape, pieces, -0.22, 0.18)
    return jnp.clip(spiked(result, jax.random.fold_in(stream_key, 3), *heavy), -bound, bound).astype(kind)


def setup_inputs(seed: int = 0) -> dict:
    seeds = jax.random.split(jax.random.key(seed), 8)
    out_grad = normal_values(seeds[0], (TOKENS, D), 1.0, 6.0, ((0, 32),))
    routes_keys = jax.random.split(jax.random.fold_in(seeds[1], 1), TOKENS // TOK_DEV)
    routes_turns = jax.random.permutation(jax.random.fold_in(seeds[1], 3), TOKENS // TOK_DEV)
    routes = jax.vmap(lambda own, number: shared_out(jax.random.fold_in(seeds[1], 2), own, number, TOK_DEV, EXPERTS, 2, MOST, 0))(routes_keys, routes_turns).reshape((TOKENS, 2))
    gates = jnp.clip(0.099609375 + 0.7988281 * jax.random.uniform(seeds[2], (TOKENS, 2), jnp.float32) ** steps_of(seeds[2], (TOKENS, 2), ((0, 32),), -0.2, 0.2), 0.099609375, 0.8984375).astype(jnp.bfloat16)
    saved_input = gaussian_with(seeds[3], (N_DP, EXPERTS, N_EXPERT, N_SEQ, MOST, D), 1.0, 6.0, ((0, 4), (1, 4)), (0, 5, 4, 2.0))
    saved_preact = normal_values(seeds[4], (N_DP, EXPERTS, N_EXPERT, N_SEQ, MOST, FF), 1.0, 6.0, ((0, 4), (1, 4), (5, 2)))
    w_in = normal_values(seeds[5], (EXPERTS, D, FF), D ** -0.5, 0.1875, ((0, 4), (2, 2)))
    w_out = normal_values(seeds[6], (EXPERTS, FF, D), FF ** -0.5, 0.125, ((0, 4), (1, 2)))
    return {"out_grad": out_grad, "routes": routes, "gates": gates, "saved_input": saved_input, "saved_preact": saved_preact, "w_in": w_in, "w_out": w_out}


def slot_targets(block_routes, experts, capacity):
    flat_routes = block_routes.reshape(-1).astype(jnp.int32)
    one_hot = (flat_routes[:, None] == jnp.arange(experts, dtype=jnp.int32)[None, :]).astype(jnp.int32)
    before = jnp.cumsum(one_hot, axis=0) - one_hot
    slot_rank = jnp.sum(before * one_hot, axis=1)
    return (flat_routes * capacity + slot_rank).reshape(block_routes.shape)


def silu_parts(preact):
    sigma = jax.nn.sigmoid(preact)
    return preact * sigma, sigma * (1.0 + preact * (1.0 - sigma))


def reference(out_grad, routes, gates, saved_input, saved_preact, w_in, w_out):
    data_groups = saved_input.shape[0]
    experts = saved_input.shape[1]
    sources = saved_input.shape[2]
    seq_groups = saved_input.shape[3]
    capacity = saved_input.shape[4]
    model_width = out_grad.shape[1]
    hidden = saved_preact.shape[5]
    block_tokens = out_grad.shape[0] // (data_groups * seq_groups * sources)
    cell_ids = jnp.arange(experts * capacity, dtype=jnp.int32)
    w_in_full = w_in.astype(jnp.float32)
    w_out_full = w_out.astype(jnp.float32)
    grads_in = out_grad.reshape(data_groups, seq_groups, sources, block_tokens, model_width)
    routes_in = routes.reshape(data_groups, seq_groups, sources, block_tokens, 2)
    gates_in = gates.reshape(data_groups, seq_groups, sources, block_tokens, 2)

    def one_group(grad_total, group_item):
        grad_block, route_block, gate_block, input_rows, preact_rows = group_item
        targets = jax.vmap(jax.vmap(lambda blk: slot_targets(blk, experts, capacity)))(route_block)
        first_pick = (targets[..., 0][..., None, :] == cell_ids[:, None]).astype(jnp.float32)
        second = (targets[..., 1][..., None, :] == cell_ids[:, None]).astype(jnp.float32)
        both_picks = first_pick + second
        row_block = jnp.einsum('abct,abtd->abcd', both_picks, grad_block.astype(jnp.float32))
        gate_cells = jnp.sum(first_pick * gate_block[..., 0][..., None, :].astype(jnp.float32)
                             + second * gate_block[..., 1][..., None, :].astype(jnp.float32), axis=-1)
        row_block = row_block.reshape(seq_groups, sources, experts, capacity, model_width)
        row_block = row_block.transpose(2, 1, 0, 3, 4).reshape(experts, -1, model_width)
        gate_cells = gate_cells.reshape(seq_groups, sources, experts, capacity)
        gate_cells = gate_cells.transpose(2, 1, 0, 3).reshape(experts, -1, 1)
        inputs_full = input_rows.reshape(experts, -1, model_width).astype(jnp.float32)
        preact_full = preact_rows.reshape(experts, -1, hidden).astype(jnp.float32)
        raw_grad = jnp.einsum('erd,efd->erf', row_block, w_out_full)
        activation, slope = silu_parts(preact_full)
        gate_slot = jnp.sum(activation * raw_grad, axis=-1).astype(jnp.bfloat16)
        delta_rows = lax.optimization_barrier((gate_cells * raw_grad * slope).astype(jnp.bfloat16))
        delta_full = delta_rows.astype(jnp.float32)
        slot_grad = lax.optimization_barrier(jnp.einsum('erf,edf->erd', delta_full, w_in_full).astype(jnp.bfloat16))
        grad_total = grad_total + jnp.einsum('erd,erf->edf', inputs_full, delta_full)
        back_rows = slot_grad.reshape(experts, sources, seq_groups, capacity, model_width)
        back_rows = back_rows.transpose(2, 1, 0, 3, 4).reshape(seq_groups, sources, experts * capacity, model_width)
        input_part = jnp.einsum('abct,abcd->abtd', both_picks, back_rows.astype(jnp.float32)).astype(jnp.bfloat16)
        gate_back = gate_slot.reshape(experts, sources, seq_groups, capacity)
        gate_back = gate_back.transpose(2, 1, 0, 3).reshape(seq_groups, sources, experts * capacity).astype(jnp.float32)
        gate_first = jnp.sum(first_pick * gate_back[..., None], axis=2)
        gate_second = jnp.sum(second * gate_back[..., None], axis=2)
        gate_part = jnp.stack([gate_first, gate_second], axis=-1).astype(jnp.bfloat16)
        return grad_total, (input_part, gate_part)

    start_total = jnp.zeros((experts, model_width, hidden), jnp.float32)
    grad_total, outputs = lax.scan(one_group, start_total,
                                   (grads_in, routes_in, gates_in, saved_input, saved_preact))
    input_grad = outputs[0].reshape(-1, model_width)
    gate_grad = outputs[1].reshape(-1, 2)
    weight_grad = grad_total * (1.0 / data_groups)
    return input_grad, gate_grad, weight_grad
```

```python
import jax
import jax.numpy as jnp
from jax import lax
from jax.sharding import PartitionSpec as P

GATE_ROWS = 8


def slot_targets(block_routes, experts, capacity):
    flat_routes = block_routes.reshape(-1)
    one_hot = (flat_routes[:, None] == jnp.arange(experts, dtype=jnp.int32)[None, :]).astype(
        jnp.int32
    )
    before = jnp.cumsum(one_hot, axis=0) - one_hot
    slot_rank = jnp.sum(before * one_hot, axis=1)
    return (flat_routes * capacity + slot_rank).reshape(block_routes.shape)


def silu_parts(preact):
    sigma = jax.nn.sigmoid(preact)
    return (preact * sigma, sigma * (1.0 + preact * (1.0 - sigma)))


def gate_block(values, model_width):
    capacity = values.shape[-1]
    lead = values.ndim - 1
    padded = jnp.pad(
        values[..., None, :],
        [(0, 0)] * lead + [(0, GATE_ROWS - 1), (0, model_width - capacity)],
    )
    return padded


def seq_swap(x):
    return lax.ppermute(x, "seq", [(0, 1), (1, 0)])


def on_device(out_grad, routes, gates, saved_input, saved_preact, w_in, w_out):
    model_width = out_grad.shape[1]
    experts = lax.axis_size("expert")
    halves = lax.axis_size("seq")
    data_groups = lax.axis_size("dp")
    capacity = saved_input.shape[4]
    rows_per = capacity + GATE_ROWS
    cell_ids = jnp.arange(experts * capacity, dtype=jnp.int32)
    targets = slot_targets(routes, experts, capacity)
    first_pick = targets[:, 0][None, :] == cell_ids[:, None]
    second = targets[:, 1][None, :] == cell_ids[:, None]
    send_matrix = (first_pick | second).astype(jnp.bfloat16)
    send_rows = jnp.dot(send_matrix, out_grad, preferred_element_type=jnp.float32)
    send_rows = send_rows.astype(jnp.bfloat16).reshape(experts, capacity, model_width)
    gate_cells = jnp.sum(
        jnp.where(first_pick, gates[:, 0][None, :].astype(jnp.float32), 0.0)
        + jnp.where(second, gates[:, 1][None, :].astype(jnp.float32), 0.0),
        axis=1,
    )
    gate_cells = gate_cells.astype(jnp.bfloat16).reshape(experts, capacity)
    payload = jnp.concatenate([send_rows, gate_block(gate_cells, model_width)], axis=1)

    if halves == 2:
        seq_pos = lax.axis_index("seq")
        other = seq_swap(payload)
        group = jnp.where(
            seq_pos == 0, jnp.stack([payload, other], axis=1), jnp.stack([other, payload], axis=1)
        )
    else:
        group = lax.all_gather(payload, "seq", axis=1, tiled=False)
    group = lax.all_to_all(group, "expert", split_axis=0, concat_axis=0, tiled=True)
    row_count = experts * halves * capacity
    flat_rows = group[:, :, :capacity, :].reshape(row_count, model_width)
    flat_gates = group[:, :, capacity, :capacity].reshape(row_count, 1).astype(jnp.float32)
    input_rows = saved_input.reshape(row_count, model_width)
    preact_rows = saved_preact.reshape(row_count, -1).astype(jnp.float32)
    w_in_half = w_in[0]
    w_out_half = w_out[0]
    raw_grad = lax.dot_general(
        flat_rows, w_out_half, (((1,), (1,)), ((), ())), preferred_element_type=jnp.float32
    )
    activation, slope = silu_parts(preact_rows)
    gate_part = jnp.sum(activation * raw_grad, axis=1)
    delta_rows = (flat_gates * raw_grad * slope).astype(jnp.bfloat16)
    weight_part = lax.dot_general(
        input_rows, delta_rows, (((0,), (0,)), ((), ())), preferred_element_type=jnp.float32
    )
    weight_share = lax.psum_scatter(
        (weight_part * (1.0 / data_groups)).astype(jnp.bfloat16),
        "dp",
        scatter_dimension=0,
        tiled=True,
    )
    weight_grad = weight_share.astype(jnp.float32)[None]
    grad_part = lax.dot_general(
        delta_rows, w_in_half, (((1,), (1,)), ((), ())), preferred_element_type=jnp.float32
    )
    back = jnp.concatenate(
        [
            grad_part.reshape(experts, halves, capacity, model_width),
            gate_block(gate_part.reshape(experts, halves, capacity), model_width),
        ],
        axis=2,
    )
    if halves == 2:
        mine = jnp.where(seq_pos == 0, back[:, 0], back[:, 1])
        theirs = jnp.where(seq_pos == 0, back[:, 1], back[:, 0])
        received = seq_swap(theirs.astype(jnp.bfloat16))
        summed = (mine + received.astype(jnp.float32)).astype(jnp.bfloat16)
    else:
        summed = lax.psum_scatter(back, "seq", scatter_dimension=1, tiled=True)
        summed = summed.reshape(experts, rows_per, model_width).astype(jnp.bfloat16)
    back_rows = lax.all_to_all(summed, "expert", split_axis=0, concat_axis=0, tiled=True)
    back_flat = back_rows[:, :capacity, :].reshape(experts * capacity, model_width)
    input_grad = lax.dot_general(
        send_matrix, back_flat, (((0,), (0,)), ((), ())), preferred_element_type=jnp.float32
    ).astype(jnp.bfloat16)
    gate_values = back_rows[:, capacity, :capacity].reshape(experts * capacity).astype(jnp.float32)
    gate_first = jnp.sum(jnp.where(first_pick, gate_values[:, None], 0.0), axis=0)
    gate_second = jnp.sum(jnp.where(second, gate_values[:, None], 0.0), axis=0)
    gate_grad = jnp.stack([gate_first, gate_second], axis=1).astype(jnp.bfloat16)
    return (input_grad, gate_grad, weight_grad)


def solution(mesh):
    return jax.shard_map(
        on_device,
        mesh=mesh,
        in_specs=(
            P(("dp", "seq", "expert"), None),
            P(("dp", "seq", "expert"), None),
            P(("dp", "seq", "expert"), None),
            P("dp", "expert", None, None, None, None),
            P("dp", "expert", None, None, None, "seq"),
            P("expert", None, "seq"),
            P("expert", "seq", None),
        ),
        out_specs=(
            P(("dp", "seq", "expert"), None),
            P(("dp", "seq", "expert"), None),
            P("expert", "dp", "seq"),
        ),
        check_vma=False,
    )
```

```python
import jax
import jax.numpy as jnp
from jax import lax
from jax.sharding import PartitionSpec as P

GATE_ROWS = 8


def slot_targets(block_routes, experts, capacity):
    flat_routes = block_routes.reshape(-1)
    one_hot = (flat_routes[:, None] == jnp.arange(experts, dtype=jnp.int32)[None, :]).astype(
        jnp.int32
    )
    before = jnp.cumsum(one_hot, axis=0) - one_hot
    slot_rank = jnp.sum(before * one_hot, axis=1)
    return (flat_routes * capacity + slot_rank).reshape(block_routes.shape)


def silu_parts(preact):
    sigma = jax.nn.sigmoid(preact)
    return (preact * sigma, sigma * (1.0 + preact * (1.0 - sigma)))


def gate_block(values, model_width):
    capacity = values.shape[-1]
    lead = values.ndim - 1
    padded = jnp.pad(
        values[..., None, :],
        [(0, 0)] * lead + [(0, GATE_ROWS - 1), (0, model_width - capacity)],
    )
    return padded


def seq_swap(x):
    return lax.ppermute(x, "seq", [(0, 1), (1, 0)])


def expert_rows(block, input_rows, preact_rows, w_in_half, w_out_half):
    sources, capacity, model_width = input_rows.shape
    count = sources * capacity
    rows = block[:, :capacity, :].reshape(count, model_width)
    row_gates = block[:, capacity, :capacity].reshape(count, 1).astype(jnp.float32)
    raw_grad = lax.dot_general(
        rows, w_out_half, (((1,), (1,)), ((), ())), preferred_element_type=jnp.float32
    )
    activation, slope = silu_parts(preact_rows.reshape(count, -1).astype(jnp.float32))
    gate_part = jnp.sum(activation * raw_grad, axis=1)
    delta_rows = (row_gates * raw_grad * slope).astype(jnp.bfloat16)
    grad_part = lax.dot_general(
        delta_rows, w_in_half, (((1,), (1,)), ((), ())), preferred_element_type=jnp.float32
    )
    back = jnp.concatenate(
        [
            grad_part.reshape(sources, capacity, model_width),
            gate_block(gate_part.reshape(sources, capacity), model_width),
        ],
        axis=1,
    )
    weight_part = lax.dot_general(
        input_rows.reshape(count, model_width),
        delta_rows,
        (((0,), (0,)), ((), ())),
        preferred_element_type=jnp.float32,
    )
    return back, weight_part


def on_device(out_grad, routes, gates, saved_input, saved_preact, w_in, w_out):
    model_width = out_grad.shape[1]
    experts = lax.axis_size("expert")
    halves = lax.axis_size("seq")
    data_groups = lax.axis_size("dp")
    capacity = saved_input.shape[4]
    cell_ids = jnp.arange(experts * capacity, dtype=jnp.int32)
    targets = slot_targets(routes, experts, capacity)
    first_pick = targets[:, 0][None, :] == cell_ids[:, None]
    second = targets[:, 1][None, :] == cell_ids[:, None]
    send_matrix = (first_pick | second).astype(jnp.bfloat16)
    send_rows = jnp.dot(send_matrix, out_grad, preferred_element_type=jnp.float32)
    send_rows = send_rows.astype(jnp.bfloat16).reshape(experts, capacity, model_width)
    gate_cells = jnp.sum(
        jnp.where(first_pick, gates[:, 0][None, :].astype(jnp.float32), 0.0)
        + jnp.where(second, gates[:, 1][None, :].astype(jnp.float32), 0.0),
        axis=1,
    )
    gate_cells = gate_cells.astype(jnp.bfloat16).reshape(experts, capacity)
    payload = jnp.concatenate([send_rows, gate_block(gate_cells, model_width)], axis=1)
    same = lax.all_to_all(payload, "expert", split_axis=0, concat_axis=0, tiled=True)
    w_in_half = w_in[0]
    w_out_half = w_out[0]
    inputs = saved_input[0, 0]
    preacts = saved_preact[0, 0]
    if halves == 2:
        seq_pos = lax.axis_index("seq")
        other = seq_swap(same)
        own_back, own_weight = expert_rows(
            same,
            lax.dynamic_index_in_dim(inputs, seq_pos, axis=1, keepdims=False),
            lax.dynamic_index_in_dim(preacts, seq_pos, axis=1, keepdims=False),
            w_in_half,
            w_out_half,
        )
        far_back, far_weight = expert_rows(
            other,
            lax.dynamic_index_in_dim(inputs, 1 - seq_pos, axis=1, keepdims=False),
            lax.dynamic_index_in_dim(preacts, 1 - seq_pos, axis=1, keepdims=False),
            w_in_half,
            w_out_half,
        )
        received = seq_swap(far_back.astype(jnp.bfloat16))
        summed = (own_back + received.astype(jnp.float32)).astype(jnp.bfloat16)
        weight_part = own_weight + far_weight
    else:
        group = lax.all_gather(same, "seq", axis=1, tiled=False)
        sources = group.shape[0]
        flat = group.reshape(sources * halves, -1, model_width)
        back, weight_part = expert_rows(
            flat,
            inputs.reshape(sources * halves, capacity, model_width),
            preacts.reshape(sources * halves, capacity, -1),
            w_in_half,
            w_out_half,
        )
        back = back.reshape(sources, halves, -1, model_width)
        summed = lax.psum_scatter(back, "seq", scatter_dimension=1, tiled=True)
        summed = summed.reshape(sources, -1, model_width).astype(jnp.bfloat16)
    weight_share = lax.psum_scatter(
        (weight_part * (1.0 / data_groups)).astype(jnp.bfloat16),
        "dp",
        scatter_dimension=0,
        tiled=True,
    )
    weight_grad = weight_share.astype(jnp.float32)[None]
    back_rows = lax.all_to_all(summed, "expert", split_axis=0, concat_axis=0, tiled=True)
    back_flat = back_rows[:, :capacity, :].reshape(experts * capacity, model_width)
    input_grad = lax.dot_general(
        send_matrix, back_flat, (((0,), (0,)), ((), ())), preferred_element_type=jnp.float32
    ).astype(jnp.bfloat16)
    gate_values = back_rows[:, capacity, :capacity].reshape(experts * capacity).astype(jnp.float32)
    gate_first = jnp.sum(jnp.where(first_pick, gate_values[:, None], 0.0), axis=0)
    gate_second = jnp.sum(jnp.where(second, gate_values[:, None], 0.0), axis=0)
    gate_grad = jnp.stack([gate_first, gate_second], axis=1).astype(jnp.bfloat16)
    return (input_grad, gate_grad, weight_grad)


def solution(mesh):
    return jax.shard_map(
        on_device,
        mesh=mesh,
        in_specs=(
            P(("dp", "seq", "expert"), None),
            P(("dp", "seq", "expert"), None),
            P(("dp", "seq", "expert"), None),
            P("dp", "expert", None, None, None, None),
            P("dp", "expert", None, None, None, "seq"),
            P("expert", None, "seq"),
            P("expert", "seq", None),
        ),
        out_specs=(
            P(("dp", "seq", "expert"), None),
            P(("dp", "seq", "expert"), None),
            P("expert", "dp", "seq"),
        ),
        check_vma=False,
    )
```

```python
import jax
import jax.numpy as jnp
from jax import lax
from jax.sharding import PartitionSpec as P

GATE_ROWS = 8


def slot_targets(block_routes, experts, capacity):
    flat_routes = block_routes.reshape(-1)
    one_hot = (flat_routes[:, None] == jnp.arange(experts, dtype=jnp.int32)[None, :]).astype(
        jnp.int32
    )
    before = jnp.cumsum(one_hot, axis=0) - one_hot
    slot_rank = jnp.sum(before * one_hot, axis=1)
    return (flat_routes * capacity + slot_rank).reshape(block_routes.shape)


def silu_parts(preact):
    sigma = jax.nn.sigmoid(preact)
    return (preact * sigma, sigma * (1.0 + preact * (1.0 - sigma)))


def gate_block(values, model_width):
    capacity = values.shape[-1]
    lead = values.ndim - 1
    padded = jnp.pad(
        values[..., None, :],
        [(0, 0)] * lead + [(0, GATE_ROWS - 1), (0, model_width - capacity)],
    )
    return padded


def seq_swap(x):
    return lax.ppermute(x, "seq", [(0, 1), (1, 0)])


def expert_rows(block, input_rows, preact_rows, w_in_half, w_out_half):
    sources, capacity, model_width = input_rows.shape
    count = sources * capacity
    rows = block[:, :capacity, :].reshape(count, model_width)
    row_gates = block[:, capacity, :capacity].reshape(count, 1).astype(jnp.float32)
    raw_grad = lax.dot_general(
        rows, w_out_half, (((1,), (1,)), ((), ())), preferred_element_type=jnp.float32
    )
    activation, slope = silu_parts(preact_rows.reshape(count, -1).astype(jnp.float32))
    gate_part = jnp.sum(activation * raw_grad, axis=1)
    delta_rows = (row_gates * raw_grad * slope).astype(jnp.bfloat16)
    grad_part = lax.dot_general(
        delta_rows, w_in_half, (((1,), (1,)), ((), ())), preferred_element_type=jnp.float32
    )
    back = jnp.concatenate(
        [
            grad_part.reshape(sources, capacity, model_width),
            gate_block(gate_part.reshape(sources, capacity), model_width),
        ],
        axis=1,
    )
    weight_part = lax.dot_general(
        input_rows.reshape(count, model_width),
        delta_rows,
        (((0,), (0,)), ((), ())),
        preferred_element_type=jnp.float32,
    )
    return back, weight_part


def on_device(out_grad, routes, gates, saved_input, saved_preact, w_in, w_out):
    model_width = out_grad.shape[1]
    experts = lax.axis_size("expert")
    halves = lax.axis_size("seq")
    data_groups = lax.axis_size("dp")
    capacity = saved_input.shape[4]
    expert_pos = lax.axis_index("expert")
    seq_pos = lax.axis_index("seq")
    rel_routes = jnp.bitwise_xor(routes, expert_pos)
    cell_ids = jnp.arange(experts * capacity, dtype=jnp.int32)
    targets = slot_targets(rel_routes, experts, capacity)
    first_pick = targets[:, 0][None, :] == cell_ids[:, None]
    second = targets[:, 1][None, :] == cell_ids[:, None]
    send_matrix = (first_pick | second).astype(jnp.bfloat16)
    send_rows = jnp.dot(send_matrix, out_grad, preferred_element_type=jnp.float32)
    send_rows = send_rows.astype(jnp.bfloat16).reshape(experts, capacity, model_width)
    gate_cells = jnp.sum(
        jnp.where(first_pick, gates[:, 0][None, :].astype(jnp.float32), 0.0)
        + jnp.where(second, gates[:, 1][None, :].astype(jnp.float32), 0.0),
        axis=1,
    )
    gate_cells = gate_cells.astype(jnp.bfloat16).reshape(experts, capacity)
    payload = jnp.concatenate([send_rows, gate_block(gate_cells, model_width)], axis=1)

    def pairs(ds, k):
        return [
            (ss * experts + jj, (ss ^ ds) * experts + (jj ^ k))
            for ss in range(halves)
            for jj in range(experts)
        ]

    received = {}
    for ds in range(halves):
        for k in range(experts):
            if ds == 0 and k == 0:
                received[(ds, k)] = payload[0]
            else:
                received[(ds, k)] = lax.ppermute(payload[k], ("seq", "expert"), pairs(ds, k))
    near = jnp.stack([received[(0, k)] for k in range(experts)])
    far = jnp.stack([received[(1, k)] for k in range(experts)])
    order = jnp.bitwise_xor(expert_pos, jnp.arange(experts, dtype=jnp.int32))
    inputs = saved_input[0, 0]
    preacts = saved_preact[0, 0]

    def saved_rows(values, seq_index):
        half = lax.dynamic_index_in_dim(values, seq_index, axis=1, keepdims=False)
        return jnp.take(half, order, axis=0)

    w_in_half = w_in[0]
    w_out_half = w_out[0]
    near_back, near_weight = expert_rows(
        near, saved_rows(inputs, seq_pos), saved_rows(preacts, seq_pos), w_in_half, w_out_half
    )
    far_back, far_weight = expert_rows(
        far, saved_rows(inputs, 1 - seq_pos), saved_rows(preacts, 1 - seq_pos), w_in_half, w_out_half
    )
    weight_share = lax.psum_scatter(
        ((near_weight + far_weight) * (1.0 / data_groups)).astype(jnp.bfloat16),
        "dp",
        scatter_dimension=0,
        tiled=True,
    )
    weight_grad = weight_share.astype(jnp.float32)[None]
    back = [None] * experts
    for k in range(experts):
        partner_part = seq_swap(far_back[k].astype(jnp.bfloat16))
        summed = (near_back[k] + partner_part.astype(jnp.float32)).astype(jnp.bfloat16)
        if k == 0:
            back[k] = summed
        else:
            back[k] = lax.ppermute(summed, "expert", [(jj, jj ^ k) for jj in range(experts)])
    back_rows = jnp.stack(back)
    back_flat = back_rows[:, :capacity, :].reshape(experts * capacity, model_width)
    input_grad = lax.dot_general(
        send_matrix, back_flat, (((0,), (0,)), ((), ())), preferred_element_type=jnp.float32
    ).astype(jnp.bfloat16)
    gate_values = back_rows[:, capacity, :capacity].reshape(experts * capacity).astype(jnp.float32)
    gate_first = jnp.sum(jnp.where(first_pick, gate_values[:, None], 0.0), axis=0)
    gate_second = jnp.sum(jnp.where(second, gate_values[:, None], 0.0), axis=0)
    gate_grad = jnp.stack([gate_first, gate_second], axis=1).astype(jnp.bfloat16)
    return (input_grad, gate_grad, weight_grad)


def solution(mesh):
    return jax.shard_map(
        on_device,
        mesh=mesh,
        in_specs=(
            P(("dp", "seq", "expert"), None),
            P(("dp", "seq", "expert"), None),
            P(("dp", "seq", "expert"), None),
            P("dp", "expert", None, None, None, None),
            P("dp", "expert", None, None, None, "seq"),
            P("expert", None, "seq"),
            P("expert", "seq", None),
        ),
        out_specs=(
            P(("dp", "seq", "expert"), None),
            P(("dp", "seq", "expert"), None),
            P("expert", "dp", "seq"),
        ),
        check_vma=False,
    )
```

```python
import jax
import jax.numpy as jnp
from jax import lax
from jax.experimental.layout import Layout, with_layout_constraint
from jax.sharding import PartitionSpec as P


GATE_ROWS = 8


def slot_targets(block_routes, experts, capacity):
    flat_routes = block_routes.reshape(-1)
    one_hot = (flat_routes[:, None] == jnp.arange(experts, dtype=jnp.int32)[None, :]).astype(
        jnp.int32
    )
    before = jnp.cumsum(one_hot, axis=0) - one_hot
    slot_rank = jnp.sum(before * one_hot, axis=1)
    return (flat_routes * capacity + slot_rank).reshape(block_routes.shape)


def silu_parts(preact):
    sigma = jax.nn.sigmoid(preact)
    return (preact * sigma, sigma * (1.0 + preact * (1.0 - sigma)))


def gate_block(values, model_width):
    capacity = values.shape[-1]
    lead = values.ndim - 1
    padded = jnp.pad(
        values[..., None, :],
        [(0, 0)] * lead + [(0, GATE_ROWS - 1), (0, model_width - capacity)],
    )
    return padded


def seq_swap(x):
    return lax.ppermute(x, "seq", [(0, 1), (1, 0)])


def expert_rows(block, input_rows, preact_rows, w_in_half, w_out_half):
    sources, capacity, model_width = input_rows.shape
    count = sources * capacity
    rows = block[:, :capacity, :].reshape(count, model_width)
    row_gates = block[:, capacity, :capacity].reshape(count, 1).astype(jnp.float32)
    raw_grad = lax.dot_general(
        rows, w_out_half, (((1,), (1,)), ((), ())), preferred_element_type=jnp.float32
    )
    activation, slope = silu_parts(preact_rows.reshape(count, -1).astype(jnp.float32))
    gate_part = jnp.sum(activation * raw_grad, axis=1)
    delta_rows = (row_gates * raw_grad * slope).astype(jnp.bfloat16)
    grad_part = lax.dot_general(
        delta_rows, w_in_half, (((1,), (1,)), ((), ())), preferred_element_type=jnp.float32
    )
    back = jnp.concatenate(
        [
            grad_part.reshape(sources, capacity, model_width),
            gate_block(gate_part.reshape(sources, capacity), model_width),
        ],
        axis=1,
    )
    weight_part = lax.dot_general(
        input_rows.reshape(count, model_width),
        delta_rows,
        (((0,), (0,)), ((), ())),
        preferred_element_type=jnp.float32,
    )
    return back, weight_part


def on_device(out_grad, routes, gates, saved_input, saved_preact, w_in, w_out):
    model_width = out_grad.shape[1]
    experts = lax.axis_size("expert")
    halves = lax.axis_size("seq")
    data_groups = lax.axis_size("dp")
    capacity = saved_input.shape[4]
    expert_pos = lax.axis_index("expert")
    seq_pos = lax.axis_index("seq")
    rel_routes = jnp.bitwise_xor(routes, expert_pos)
    cell_ids = jnp.arange(experts * capacity, dtype=jnp.int32)
    targets = slot_targets(rel_routes, experts, capacity)
    first_pick = targets[:, 0][None, :] == cell_ids[:, None]
    second = targets[:, 1][None, :] == cell_ids[:, None]
    send_matrix = (first_pick | second).astype(jnp.bfloat16)
    send_rows = jnp.dot(send_matrix, out_grad, preferred_element_type=jnp.float32)
    send_rows = send_rows.astype(jnp.bfloat16).reshape(experts, capacity, model_width)
    gate_cells = jnp.sum(
        jnp.where(first_pick, gates[:, 0][None, :].astype(jnp.float32), 0.0)
        + jnp.where(second, gates[:, 1][None, :].astype(jnp.float32), 0.0),
        axis=1,
    )
    gate_cells = gate_cells.astype(jnp.bfloat16).reshape(experts, capacity)
    payload = jnp.concatenate([send_rows, gate_block(gate_cells, model_width)], axis=1)

    def pairs(ds, k):
        return [
            (ss * experts + jj, (ss ^ ds) * experts + (jj ^ k))
            for ss in range(halves)
            for jj in range(experts)
        ]

    received = {}
    for ds in range(halves):
        for k in range(experts):
            if ds == 0 and k == 0:
                received[(ds, k)] = payload[0]
            else:
                received[(ds, k)] = lax.ppermute(payload[k], ("seq", "expert"), pairs(ds, k))
    near = jnp.stack([received[(0, k)] for k in range(experts)])
    far = jnp.stack([received[(1, k)] for k in range(experts)])
    order = jnp.bitwise_xor(expert_pos, jnp.arange(experts, dtype=jnp.int32))
    inputs = saved_input[0, 0]
    preacts = saved_preact[0, 0]

    def saved_rows(values, seq_index):
        half = lax.dynamic_index_in_dim(values, seq_index, axis=1, keepdims=False)
        return jnp.take(half, order, axis=0)

    w_in_half = w_in[0]
    w_out_half = w_out[0]
    near_back, near_weight = expert_rows(
        near, saved_rows(inputs, seq_pos), saved_rows(preacts, seq_pos), w_in_half, w_out_half
    )
    far_back, far_weight = expert_rows(
        far, saved_rows(inputs, 1 - seq_pos), saved_rows(preacts, 1 - seq_pos), w_in_half, w_out_half
    )
    weight_part = ((near_weight + far_weight) * (1.0 / data_groups)).astype(jnp.bfloat16)
    weight_part = with_layout_constraint(weight_part, Layout(major_to_minor=(0, 1)))
    weight_share = lax.psum_scatter(
        weight_part,
        "dp",
        scatter_dimension=0,
        tiled=True,
    )
    weight_grad = weight_share.astype(jnp.float32)[None]
    back = [None] * experts
    for k in range(experts):
        partner_part = seq_swap(far_back[k].astype(jnp.bfloat16))
        summed = (near_back[k] + partner_part.astype(jnp.float32)).astype(jnp.bfloat16)
        if k == 0:
            back[k] = summed
        else:
            back[k] = lax.ppermute(summed, "expert", [(jj, jj ^ k) for jj in range(experts)])
    back_rows = jnp.stack(back)
    back_flat = back_rows[:, :capacity, :].reshape(experts * capacity, model_width)
    input_grad = lax.dot_general(
        send_matrix, back_flat, (((0,), (0,)), ((), ())), preferred_element_type=jnp.float32
    ).astype(jnp.bfloat16)
    gate_values = back_rows[:, capacity, :capacity].reshape(experts * capacity).astype(jnp.float32)
    gate_first = jnp.sum(jnp.where(first_pick, gate_values[:, None], 0.0), axis=0)
    gate_second = jnp.sum(jnp.where(second, gate_values[:, None], 0.0), axis=0)
    gate_grad = jnp.stack([gate_first, gate_second], axis=1).astype(jnp.bfloat16)
    return (input_grad, gate_grad, weight_grad)


def solution(mesh):
    return jax.shard_map(
        on_device,
        mesh=mesh,
        in_specs=(
            P(("dp", "seq", "expert"), None),
            P(("dp", "seq", "expert"), None),
            P(("dp", "seq", "expert"), None),
            P("dp", "expert", None, None, None, None),
            P("dp", "expert", None, None, None, "seq"),
            P("expert", None, "seq"),
            P("expert", "seq", None),
        ),
        out_specs=(
            P(("dp", "seq", "expert"), None),
            P(("dp", "seq", "expert"), None),
            P("expert", "dp", "seq"),
        ),
        check_vma=False,
    )
```

```python
import jax
import jax.numpy as jnp
from jax import lax
from jax.experimental.layout import Layout, with_layout_constraint
from jax.sharding import PartitionSpec as P


GATE_ROWS = 8


def slot_targets(block_routes, experts, capacity):
    flat_routes = block_routes.reshape(-1)
    one_hot = (flat_routes[:, None] == jnp.arange(experts, dtype=jnp.int32)[None, :]).astype(
        jnp.int32
    )
    before = jnp.cumsum(one_hot, axis=0) - one_hot
    slot_rank = jnp.sum(before * one_hot, axis=1)
    return (flat_routes * capacity + slot_rank).reshape(block_routes.shape)


def silu_parts(preact):
    sigma = jax.nn.sigmoid(preact)
    return (preact * sigma, sigma * (1.0 + preact * (1.0 - sigma)))


def gate_block(values, model_width):
    capacity = values.shape[-1]
    lead = values.ndim - 1
    padded = jnp.pad(
        values[..., None, :],
        [(0, 0)] * lead + [(0, GATE_ROWS - 1), (0, model_width - capacity)],
    )
    return padded


def seq_swap(x):
    return lax.ppermute(x, "seq", [(0, 1), (1, 0)])


def expert_rows(block, input_rows, preact_rows, w_in_half, w_out_half):
    sources, capacity, model_width = input_rows.shape
    count = sources * capacity
    rows = block[:, :capacity, :].reshape(count, model_width)
    row_gates = block[:, capacity, :capacity].reshape(count, 1).astype(jnp.float32)
    raw_grad = lax.dot_general(
        rows, w_out_half, (((1,), (1,)), ((), ())), preferred_element_type=jnp.float32
    )
    activation, slope = silu_parts(preact_rows.reshape(count, -1).astype(jnp.float32))
    gate_part = jnp.sum(activation * raw_grad, axis=1)
    delta_rows = (row_gates * raw_grad * slope).astype(jnp.bfloat16)
    grad_part = lax.dot_general(
        delta_rows, w_in_half, (((1,), (1,)), ((), ())), preferred_element_type=jnp.float32
    )
    back = jnp.concatenate(
        [
            grad_part.reshape(sources, capacity, model_width),
            gate_block(gate_part.reshape(sources, capacity), model_width),
        ],
        axis=1,
    )
    weight_part = lax.dot_general(
        input_rows.reshape(count, model_width),
        delta_rows,
        (((0,), (0,)), ((), ())),
        preferred_element_type=jnp.float32,
    )
    return back, weight_part


def on_device(out_grad, routes, gates, saved_input, saved_preact, w_in, w_out):
    model_width = out_grad.shape[1]
    experts = lax.axis_size("expert")
    halves = lax.axis_size("seq")
    data_groups = lax.axis_size("dp")
    capacity = saved_input.shape[4]
    expert_pos = lax.axis_index("expert")
    seq_pos = lax.axis_index("seq")
    rel_routes = jnp.bitwise_xor(routes, expert_pos)
    cell_ids = jnp.arange(experts * capacity, dtype=jnp.int32)
    targets = slot_targets(rel_routes, experts, capacity)
    first_pick = targets[:, 0][None, :] == cell_ids[:, None]
    second = targets[:, 1][None, :] == cell_ids[:, None]
    send_matrix = (first_pick | second).astype(jnp.bfloat16)
    send_rows = jnp.dot(send_matrix, out_grad, preferred_element_type=jnp.float32)
    send_rows = send_rows.astype(jnp.bfloat16).reshape(experts, capacity, model_width)
    gate_cells = jnp.sum(
        jnp.where(first_pick, gates[:, 0][None, :].astype(jnp.float32), 0.0)
        + jnp.where(second, gates[:, 1][None, :].astype(jnp.float32), 0.0),
        axis=1,
    )
    gate_cells = gate_cells.astype(jnp.bfloat16).reshape(experts, capacity)
    payload = jnp.concatenate([send_rows, gate_block(gate_cells, model_width)], axis=1)

    def pairs(ds, k):
        return [
            (ss * experts + jj, (ss ^ ds) * experts + (jj ^ k))
            for ss in range(halves)
            for jj in range(experts)
        ]

    received = {}
    for ds in range(halves):
        for k in range(experts):
            if ds == 0 and k == 0:
                received[(ds, k)] = payload[0]
            else:
                received[(ds, k)] = lax.ppermute(payload[k], ("seq", "expert"), pairs(ds, k))
    by_offset = jnp.stack(
        [jnp.stack([received[(ds, k)] for k in range(experts)]) for ds in range(halves)]
    )
    order = jnp.bitwise_xor(expert_pos, jnp.arange(experts, dtype=jnp.int32))
    seq_order = jnp.bitwise_xor(seq_pos, jnp.arange(halves, dtype=jnp.int32))
    natural = by_offset[seq_order[None, :], order[:, None]]
    rows_per = natural.shape[2]
    all_back, weight_part = expert_rows(
        natural.reshape(experts * halves, rows_per, model_width),
        saved_input[0, 0].reshape(experts * halves, capacity, model_width),
        saved_preact[0, 0].reshape(experts * halves, capacity, -1),
        w_in[0],
        w_out[0],
    )
    weight_part = (weight_part * (1.0 / data_groups)).astype(jnp.bfloat16)
    weight_part = with_layout_constraint(weight_part, Layout(major_to_minor=(0, 1)))
    weight_share = lax.psum_scatter(weight_part, "dp", scatter_dimension=0, tiled=True)
    weight_grad = weight_share.astype(jnp.float32)[None]
    all_back = all_back.reshape(experts, halves, rows_per, model_width)
    mine = lax.dynamic_index_in_dim(all_back, seq_pos, axis=1, keepdims=False)
    theirs = lax.dynamic_index_in_dim(all_back, 1 - seq_pos, axis=1, keepdims=False)
    partner_part = seq_swap(theirs.astype(jnp.bfloat16))
    summed = (mine + partner_part.astype(jnp.float32)).astype(jnp.bfloat16)
    summed = jnp.take(summed, order, axis=0)
    back = [summed[0]] + [
        lax.ppermute(summed[k], "expert", [(jj, jj ^ k) for jj in range(experts)])
        for k in range(1, experts)
    ]
    back_rows = jnp.stack(back)
    back_flat = back_rows[:, :capacity, :].reshape(experts * capacity, model_width)
    input_grad = lax.dot_general(
        send_matrix, back_flat, (((0,), (0,)), ((), ())), preferred_element_type=jnp.float32
    ).astype(jnp.bfloat16)
    gate_values = back_rows[:, capacity, :capacity].reshape(experts * capacity).astype(jnp.float32)
    gate_first = jnp.sum(jnp.where(first_pick, gate_values[:, None], 0.0), axis=0)
    gate_second = jnp.sum(jnp.where(second, gate_values[:, None], 0.0), axis=0)
    gate_grad = jnp.stack([gate_first, gate_second], axis=1).astype(jnp.bfloat16)
    return (input_grad, gate_grad, weight_grad)


def solution(mesh):
    return jax.shard_map(
        on_device,
        mesh=mesh,
        in_specs=(
            P(("dp", "seq", "expert"), None),
            P(("dp", "seq", "expert"), None),
            P(("dp", "seq", "expert"), None),
            P("dp", "expert", None, None, None, None),
            P("dp", "expert", None, None, None, "seq"),
            P("expert", None, "seq"),
            P("expert", "seq", None),
        ),
        out_specs=(
            P(("dp", "seq", "expert"), None),
            P(("dp", "seq", "expert"), None),
            P("expert", "dp", "seq"),
        ),
        check_vma=False,
    )
```

```python
import jax
import jax.numpy as jnp
from jax import lax
from jax.experimental.layout import Layout, with_layout_constraint
from jax.sharding import PartitionSpec as P


GATE_ROWS = 8


def slot_targets(block_routes, experts, capacity):
    flat_routes = block_routes.reshape(-1)
    one_hot = (flat_routes[:, None] == jnp.arange(experts, dtype=jnp.int32)[None, :]).astype(
        jnp.int32
    )
    before = jnp.cumsum(one_hot, axis=0) - one_hot
    slot_rank = jnp.sum(before * one_hot, axis=1)
    return (flat_routes * capacity + slot_rank).reshape(block_routes.shape)


def silu_parts(preact):
    sigma = jax.nn.sigmoid(preact)
    return (preact * sigma, sigma * (1.0 + preact * (1.0 - sigma)))


def gate_block(values, model_width):
    capacity = values.shape[-1]
    lead = values.ndim - 1
    padded = jnp.pad(
        values[..., None, :],
        [(0, 0)] * lead + [(0, GATE_ROWS - 1), (0, model_width - capacity)],
    )
    return padded


def seq_swap(x):
    return lax.ppermute(x, "seq", [(0, 1), (1, 0)])


def expert_rows(block, input_rows, preact_rows, w_in_half, w_out_half):
    sources, capacity, model_width = input_rows.shape
    count = sources * capacity
    rows = block[:, :capacity, :].reshape(count, model_width)
    row_gates = block[:, capacity, :capacity].reshape(count, 1).astype(jnp.float32)
    raw_grad = lax.dot_general(
        rows, w_out_half, (((1,), (1,)), ((), ())), preferred_element_type=jnp.float32
    )
    activation, slope = silu_parts(preact_rows.reshape(count, -1).astype(jnp.float32))
    gate_part = jnp.sum(activation * raw_grad, axis=1)
    delta_rows = (row_gates * raw_grad * slope).astype(jnp.bfloat16)
    grad_part = lax.dot_general(
        delta_rows, w_in_half, (((1,), (1,)), ((), ())), preferred_element_type=jnp.float32
    )
    back = jnp.concatenate(
        [
            grad_part.reshape(sources, capacity, model_width),
            gate_block(gate_part.reshape(sources, capacity), model_width),
        ],
        axis=1,
    )
    weight_part = lax.dot_general(
        input_rows.reshape(count, model_width),
        delta_rows,
        (((0,), (0,)), ((), ())),
        preferred_element_type=jnp.float32,
    )
    return back, weight_part


def line_reduce_scatter(part, axis):
    n = lax.axis_size(axis)
    if n > 8:
        return lax.psum_scatter(part.astype(jnp.bfloat16), axis, scatter_dimension=0, tiled=True).astype(jnp.float32)
    pos = lax.axis_index(axis)
    blocks = part.reshape(n, part.shape[0] // n, part.shape[1])
    up = None
    down = None
    for r in range(1, n):
        b_up = jnp.clip(n - r + pos, 0, n - 1)
        send_up = lax.dynamic_index_in_dim(blocks, b_up, axis=0, keepdims=False)
        if up is not None:
            send_up = send_up + up.astype(jnp.float32)
        up = lax.ppermute(send_up.astype(jnp.bfloat16), axis, [(i, i + 1) for i in range(r)])
        b_down = jnp.clip(pos + r - n, 0, n - 1)
        send_down = lax.dynamic_index_in_dim(blocks, b_down, axis=0, keepdims=False)
        if down is not None:
            send_down = send_down + down.astype(jnp.float32)
        down = lax.ppermute(
            send_down.astype(jnp.bfloat16), axis, [(i, i - 1) for i in range(n - r, n)]
        )
    own = lax.dynamic_index_in_dim(blocks, pos, axis=0, keepdims=False)
    if up is None:
        return own
    return own + up.astype(jnp.float32) + down.astype(jnp.float32)


def on_device(out_grad, routes, gates, saved_input, saved_preact, w_in, w_out):
    model_width = out_grad.shape[1]
    experts = lax.axis_size("expert")
    halves = lax.axis_size("seq")
    data_groups = lax.axis_size("dp")
    capacity = saved_input.shape[4]
    expert_pos = lax.axis_index("expert")
    seq_pos = lax.axis_index("seq")
    rel_routes = jnp.bitwise_xor(routes, expert_pos)
    cell_ids = jnp.arange(experts * capacity, dtype=jnp.int32)
    targets = slot_targets(rel_routes, experts, capacity)
    first_pick = targets[:, 0][None, :] == cell_ids[:, None]
    second = targets[:, 1][None, :] == cell_ids[:, None]
    send_matrix = (first_pick | second).astype(jnp.bfloat16)
    send_rows = jnp.dot(send_matrix, out_grad, preferred_element_type=jnp.float32)
    send_rows = send_rows.astype(jnp.bfloat16).reshape(experts, capacity, model_width)
    gate_cells = jnp.sum(
        jnp.where(first_pick, gates[:, 0][None, :].astype(jnp.float32), 0.0)
        + jnp.where(second, gates[:, 1][None, :].astype(jnp.float32), 0.0),
        axis=1,
    )
    gate_cells = gate_cells.astype(jnp.bfloat16).reshape(experts, capacity)
    payload = jnp.concatenate([send_rows, gate_block(gate_cells, model_width)], axis=1)

    def pairs(ds, k):
        return [
            (ss * experts + jj, (ss ^ ds) * experts + (jj ^ k))
            for ss in range(halves)
            for jj in range(experts)
        ]

    received = {}
    for ds in range(halves):
        for k in range(experts):
            if ds == 0 and k == 0:
                received[(ds, k)] = payload[0]
            else:
                received[(ds, k)] = lax.ppermute(payload[k], ("seq", "expert"), pairs(ds, k))
    by_offset = jnp.stack(
        [jnp.stack([received[(ds, k)] for k in range(experts)]) for ds in range(halves)]
    )
    order = jnp.bitwise_xor(expert_pos, jnp.arange(experts, dtype=jnp.int32))
    seq_order = jnp.bitwise_xor(seq_pos, jnp.arange(halves, dtype=jnp.int32))
    natural = by_offset[seq_order[None, :], order[:, None]]
    rows_per = natural.shape[2]
    all_back, weight_part = expert_rows(
        natural.reshape(experts * halves, rows_per, model_width),
        saved_input[0, 0].reshape(experts * halves, capacity, model_width),
        saved_preact[0, 0].reshape(experts * halves, capacity, -1),
        w_in[0],
        w_out[0],
    )
    weight_grad = line_reduce_scatter(weight_part * (1.0 / data_groups), "dp")[None]
    all_back = all_back.reshape(experts, halves, rows_per, model_width)
    mine = lax.dynamic_index_in_dim(all_back, seq_pos, axis=1, keepdims=False)
    theirs = lax.dynamic_index_in_dim(all_back, 1 - seq_pos, axis=1, keepdims=False)
    partner_part = seq_swap(theirs.astype(jnp.bfloat16))
    summed = (mine + partner_part.astype(jnp.float32)).astype(jnp.bfloat16)
    summed = jnp.take(summed, order, axis=0)
    back = [summed[0]] + [
        lax.ppermute(summed[k], "expert", [(jj, jj ^ k) for jj in range(experts)])
        for k in range(1, experts)
    ]
    back_rows = jnp.stack(back)
    back_flat = back_rows[:, :capacity, :].reshape(experts * capacity, model_width)
    input_grad = lax.dot_general(
        send_matrix, back_flat, (((0,), (0,)), ((), ())), preferred_element_type=jnp.float32
    ).astype(jnp.bfloat16)
    gate_values = back_rows[:, capacity, :capacity].reshape(experts * capacity).astype(jnp.float32)
    gate_first = jnp.sum(jnp.where(first_pick, gate_values[:, None], 0.0), axis=0)
    gate_second = jnp.sum(jnp.where(second, gate_values[:, None], 0.0), axis=0)
    gate_grad = jnp.stack([gate_first, gate_second], axis=1).astype(jnp.bfloat16)
    return (input_grad, gate_grad, weight_grad)


def solution(mesh):
    return jax.shard_map(
        on_device,
        mesh=mesh,
        in_specs=(
            P(("dp", "seq", "expert"), None),
            P(("dp", "seq", "expert"), None),
            P(("dp", "seq", "expert"), None),
            P("dp", "expert", None, None, None, None),
            P("dp", "expert", None, None, None, "seq"),
            P("expert", None, "seq"),
            P("expert", "seq", None),
        ),
        out_specs=(
            P(("dp", "seq", "expert"), None),
            P(("dp", "seq", "expert"), None),
            P("expert", "dp", "seq"),
        ),
        check_vma=False,
    )
```

```python
import jax
import jax.numpy as jnp
from jax import lax
from jax.experimental.layout import Layout, with_layout_constraint
from jax.sharding import PartitionSpec as P


GATE_ROWS = 8


def slot_targets(block_routes, experts, capacity):
    flat_routes = block_routes.reshape(-1)
    one_hot = (flat_routes[:, None] == jnp.arange(experts, dtype=jnp.int32)[None, :]).astype(
        jnp.int32
    )
    before = jnp.cumsum(one_hot, axis=0) - one_hot
    slot_rank = jnp.sum(before * one_hot, axis=1)
    return (flat_routes * capacity + slot_rank).reshape(block_routes.shape)


def silu_parts(preact):
    sigma = jax.nn.sigmoid(preact)
    return (preact * sigma, sigma * (1.0 + preact * (1.0 - sigma)))


def gate_block(values, model_width):
    capacity = values.shape[-1]
    lead = values.ndim - 1
    padded = jnp.pad(
        values[..., None, :],
        [(0, 0)] * lead + [(0, GATE_ROWS - 1), (0, model_width - capacity)],
    )
    return padded


def seq_swap(x):
    return lax.ppermute(x, "seq", [(0, 1), (1, 0)])


def expert_rows(block, input_rows, preact_rows, w_in_half, w_out_half):
    sources, capacity, model_width = input_rows.shape
    count = sources * capacity
    rows = block[:, :capacity, :].reshape(count, model_width)
    row_gates = block[:, capacity, :capacity].reshape(count, 1).astype(jnp.float32)
    raw_grad = lax.dot_general(
        rows, w_out_half, (((1,), (1,)), ((), ())), preferred_element_type=jnp.float32
    )
    activation, slope = silu_parts(preact_rows.reshape(count, -1).astype(jnp.float32))
    gate_part = jnp.sum(activation * raw_grad, axis=1)
    delta_rows = (row_gates * raw_grad * slope).astype(jnp.bfloat16)
    grad_part = lax.dot_general(
        delta_rows, w_in_half, (((1,), (1,)), ((), ())), preferred_element_type=jnp.float32
    )
    back = jnp.concatenate(
        [
            grad_part.reshape(sources, capacity, model_width),
            gate_block(gate_part.reshape(sources, capacity), model_width),
        ],
        axis=1,
    )
    weight_part = lax.dot_general(
        input_rows.reshape(count, model_width),
        delta_rows,
        (((0,), (0,)), ((), ())),
        preferred_element_type=jnp.float32,
    )
    return back, weight_part


def on_device(out_grad, routes, gates, saved_input, saved_preact, w_in, w_out):
    model_width = out_grad.shape[1]
    experts = lax.axis_size("expert")
    halves = lax.axis_size("seq")
    data_groups = lax.axis_size("dp")
    capacity = saved_input.shape[4]
    expert_pos = lax.axis_index("expert")
    seq_pos = lax.axis_index("seq")
    rel_routes = jnp.bitwise_xor(routes, expert_pos)
    cell_ids = jnp.arange(experts * capacity, dtype=jnp.int32)
    targets = slot_targets(rel_routes, experts, capacity)
    first_pick = targets[:, 0][None, :] == cell_ids[:, None]
    second = targets[:, 1][None, :] == cell_ids[:, None]
    send_matrix = (first_pick | second).astype(jnp.bfloat16)
    send_rows = jnp.dot(send_matrix, out_grad, preferred_element_type=jnp.float32)
    send_rows = send_rows.astype(jnp.bfloat16).reshape(experts, capacity, model_width)
    gate_cells = jnp.sum(
        jnp.where(first_pick, gates[:, 0][None, :].astype(jnp.float32), 0.0)
        + jnp.where(second, gates[:, 1][None, :].astype(jnp.float32), 0.0),
        axis=1,
    )
    gate_cells = gate_cells.astype(jnp.bfloat16).reshape(experts, capacity)
    payload = jnp.concatenate([send_rows, gate_block(gate_cells, model_width)], axis=1)

    def pairs(ds, k):
        return [
            (ss * experts + jj, (ss ^ ds) * experts + (jj ^ k))
            for ss in range(halves)
            for jj in range(experts)
        ]

    received = {}
    for ds in range(halves):
        for k in range(experts):
            if ds == 0 and k == 0:
                received[(ds, k)] = payload[0]
            else:
                received[(ds, k)] = lax.ppermute(payload[k], ("seq", "expert"), pairs(ds, k))
    by_offset = jnp.stack(
        [jnp.stack([received[(ds, k)] for k in range(experts)]) for ds in range(halves)]
    )
    order = jnp.bitwise_xor(expert_pos, jnp.arange(experts, dtype=jnp.int32))
    seq_order = jnp.bitwise_xor(seq_pos, jnp.arange(halves, dtype=jnp.int32))
    natural = by_offset[seq_order[None, :], order[:, None]]
    rows_per = natural.shape[2]
    all_back, weight_part = expert_rows(
        natural.reshape(experts * halves, rows_per, model_width),
        saved_input[0, 0].reshape(experts * halves, capacity, model_width),
        saved_preact[0, 0].reshape(experts * halves, capacity, -1),
        w_in[0],
        w_out[0],
    )
    weight_part = (weight_part * (1.0 / data_groups)).astype(jnp.bfloat16)
    weight_part = with_layout_constraint(weight_part, Layout(major_to_minor=(0, 1)))
    weight_blocks = lax.all_to_all(weight_part, "dp", split_axis=0, concat_axis=0, tiled=True)
    weight_blocks = weight_blocks.reshape(data_groups, -1, weight_blocks.shape[1])
    weight_grad = jnp.sum(weight_blocks.astype(jnp.float32), axis=0)[None]
    all_back = all_back.reshape(experts, halves, rows_per, model_width)
    mine = lax.dynamic_index_in_dim(all_back, seq_pos, axis=1, keepdims=False)
    theirs = lax.dynamic_index_in_dim(all_back, 1 - seq_pos, axis=1, keepdims=False)
    partner_part = seq_swap(theirs.astype(jnp.bfloat16))
    summed = (mine + partner_part.astype(jnp.float32)).astype(jnp.bfloat16)
    summed = jnp.take(summed, order, axis=0)
    back = [summed[0]] + [
        lax.ppermute(summed[k], "expert", [(jj, jj ^ k) for jj in range(experts)])
        for k in range(1, experts)
    ]
    back_rows = jnp.stack(back)
    back_flat = back_rows[:, :capacity, :].reshape(experts * capacity, model_width)
    input_grad = lax.dot_general(
        send_matrix, back_flat, (((0,), (0,)), ((), ())), preferred_element_type=jnp.float32
    ).astype(jnp.bfloat16)
    gate_values = back_rows[:, capacity, :capacity].reshape(experts * capacity).astype(jnp.float32)
    gate_first = jnp.sum(jnp.where(first_pick, gate_values[:, None], 0.0), axis=0)
    gate_second = jnp.sum(jnp.where(second, gate_values[:, None], 0.0), axis=0)
    gate_grad = jnp.stack([gate_first, gate_second], axis=1).astype(jnp.bfloat16)
    return (input_grad, gate_grad, weight_grad)


def solution(mesh):
    return jax.shard_map(
        on_device,
        mesh=mesh,
        in_specs=(
            P(("dp", "seq", "expert"), None),
            P(("dp", "seq", "expert"), None),
            P(("dp", "seq", "expert"), None),
            P("dp", "expert", None, None, None, None),
            P("dp", "expert", None, None, None, "seq"),
            P("expert", None, "seq"),
            P("expert", "seq", None),
        ),
        out_specs=(
            P(("dp", "seq", "expert"), None),
            P(("dp", "seq", "expert"), None),
            P("expert", "dp", "seq"),
        ),
        check_vma=False,
    )
```

```python
import jax
import jax.numpy as jnp
from jax import lax
from jax.experimental.layout import Layout, with_layout_constraint
from jax.sharding import PartitionSpec as P


GATE_ROWS = 8


def slot_targets(block_routes, experts, capacity):
    flat_routes = block_routes.reshape(-1)
    pairs = flat_routes.shape[0]
    one_hot = (flat_routes[:, None] == jnp.arange(experts, dtype=jnp.int32)[None, :]).astype(
        jnp.bfloat16
    )
    earlier = (
        jnp.arange(pairs, dtype=jnp.int32)[None, :] < jnp.arange(pairs, dtype=jnp.int32)[:, None]
    ).astype(jnp.bfloat16)
    before = jnp.dot(earlier, one_hot, preferred_element_type=jnp.float32)
    slot_rank = jnp.sum(before * one_hot.astype(jnp.float32), axis=1).astype(jnp.int32)
    return (flat_routes * capacity + slot_rank).reshape(block_routes.shape)


def silu_parts(preact):
    sigma = jax.nn.sigmoid(preact)
    return (preact * sigma, sigma * (1.0 + preact * (1.0 - sigma)))


def gate_block(values, model_width):
    capacity = values.shape[-1]
    lead = values.ndim - 1
    padded = jnp.pad(
        values[..., None, :],
        [(0, 0)] * lead + [(0, GATE_ROWS - 1), (0, model_width - capacity)],
    )
    return padded


def seq_swap(x):
    return lax.ppermute(x, "seq", [(0, 1), (1, 0)])


def expert_rows(block, input_rows, preact_rows, w_in_half, w_out_half):
    sources, capacity, model_width = input_rows.shape
    count = sources * capacity
    rows = block[:, :capacity, :].reshape(count, model_width)
    row_gates = block[:, capacity, :capacity].reshape(count, 1).astype(jnp.float32)
    raw_grad = lax.dot_general(
        rows, w_out_half, (((1,), (1,)), ((), ())), preferred_element_type=jnp.float32
    )
    activation, slope = silu_parts(preact_rows.reshape(count, -1).astype(jnp.float32))
    gate_part = jnp.sum(activation * raw_grad, axis=1)
    delta_rows = (row_gates * raw_grad * slope).astype(jnp.bfloat16)
    grad_part = lax.dot_general(
        delta_rows, w_in_half, (((1,), (1,)), ((), ())), preferred_element_type=jnp.float32
    )
    back = jnp.concatenate(
        [
            grad_part.reshape(sources, capacity, model_width),
            gate_block(gate_part.reshape(sources, capacity), model_width),
        ],
        axis=1,
    )
    weight_part = lax.dot_general(
        input_rows.reshape(count, model_width),
        delta_rows,
        (((0,), (0,)), ((), ())),
        preferred_element_type=jnp.float32,
    )
    return back, weight_part


def on_device(out_grad, routes, gates, saved_input, saved_preact, w_in, w_out):
    model_width = out_grad.shape[1]
    experts = lax.axis_size("expert")
    halves = lax.axis_size("seq")
    data_groups = lax.axis_size("dp")
    capacity = saved_input.shape[4]
    expert_pos = lax.axis_index("expert")
    seq_pos = lax.axis_index("seq")
    rel_routes = jnp.bitwise_xor(routes, expert_pos)
    cell_ids = jnp.arange(experts * capacity, dtype=jnp.int32)
    targets = slot_targets(rel_routes, experts, capacity)
    first_pick = targets[:, 0][None, :] == cell_ids[:, None]
    second = targets[:, 1][None, :] == cell_ids[:, None]
    send_matrix = (first_pick | second).astype(jnp.bfloat16)
    send_rows = jnp.dot(send_matrix, out_grad, preferred_element_type=jnp.float32)
    send_rows = send_rows.astype(jnp.bfloat16).reshape(experts, capacity, model_width)
    gate_cells = jnp.sum(
        jnp.where(first_pick, gates[:, 0][None, :].astype(jnp.float32), 0.0)
        + jnp.where(second, gates[:, 1][None, :].astype(jnp.float32), 0.0),
        axis=1,
    )
    gate_cells = gate_cells.astype(jnp.bfloat16).reshape(experts, capacity)
    payload = jnp.concatenate([send_rows, gate_block(gate_cells, model_width)], axis=1)

    def pairs(ds, k):
        return [
            (ss * experts + jj, (ss ^ ds) * experts + (jj ^ k))
            for ss in range(halves)
            for jj in range(experts)
        ]

    received = {}
    for ds in range(halves):
        for k in range(experts):
            if ds == 0 and k == 0:
                received[(ds, k)] = payload[0]
            else:
                received[(ds, k)] = lax.ppermute(payload[k], ("seq", "expert"), pairs(ds, k))
    by_offset = jnp.stack(
        [jnp.stack([received[(ds, k)] for k in range(experts)]) for ds in range(halves)]
    )
    order = jnp.bitwise_xor(expert_pos, jnp.arange(experts, dtype=jnp.int32))
    seq_order = jnp.bitwise_xor(seq_pos, jnp.arange(halves, dtype=jnp.int32))
    rows_per = by_offset.shape[2]
    inputs = saved_input[0, 0][order[None, :], seq_order[:, None]]
    preacts = saved_preact[0, 0][order[None, :], seq_order[:, None]]
    all_back, weight_part = expert_rows(
        by_offset.reshape(experts * halves, rows_per, model_width),
        inputs.reshape(experts * halves, capacity, model_width),
        preacts.reshape(experts * halves, capacity, -1),
        w_in[0],
        w_out[0],
    )
    weight_part = (weight_part * (1.0 / data_groups)).astype(jnp.bfloat16)
    weight_part = with_layout_constraint(weight_part, Layout(major_to_minor=(0, 1)))
    weight_blocks = lax.all_to_all(weight_part, "dp", split_axis=0, concat_axis=0, tiled=True)
    weight_blocks = weight_blocks.reshape(data_groups, -1, weight_blocks.shape[1])
    weight_grad = jnp.sum(weight_blocks.astype(jnp.float32), axis=0)[None]
    all_back = all_back.reshape(halves, experts, rows_per, model_width)
    partner_part = seq_swap(all_back[1].astype(jnp.bfloat16))
    summed = (all_back[0] + partner_part.astype(jnp.float32)).astype(jnp.bfloat16)
    back = [summed[0]] + [
        lax.ppermute(summed[k], "expert", [(jj, jj ^ k) for jj in range(experts)])
        for k in range(1, experts)
    ]
    back_rows = jnp.stack(back)
    back_flat = back_rows[:, :capacity, :].reshape(experts * capacity, model_width)
    input_grad = lax.dot_general(
        send_matrix, back_flat, (((0,), (0,)), ((), ())), preferred_element_type=jnp.float32
    ).astype(jnp.bfloat16)
    gate_values = back_rows[:, capacity, :capacity].reshape(experts * capacity).astype(jnp.float32)
    gate_first = jnp.sum(jnp.where(first_pick, gate_values[:, None], 0.0), axis=0)
    gate_second = jnp.sum(jnp.where(second, gate_values[:, None], 0.0), axis=0)
    gate_grad = jnp.stack([gate_first, gate_second], axis=1).astype(jnp.bfloat16)
    return (input_grad, gate_grad, weight_grad)


def solution(mesh):
    return jax.shard_map(
        on_device,
        mesh=mesh,
        in_specs=(
            P(("dp", "seq", "expert"), None),
            P(("dp", "seq", "expert"), None),
            P(("dp", "seq", "expert"), None),
            P("dp", "expert", None, None, None, None),
            P("dp", "expert", None, None, None, "seq"),
            P("expert", None, "seq"),
            P("expert", "seq", None),
        ),
        out_specs=(
            P(("dp", "seq", "expert"), None),
            P(("dp", "seq", "expert"), None),
            P("expert", "dp", "seq"),
        ),
        check_vma=False,
    )
```

```python
import jax
import jax.numpy as jnp
from jax import lax
from jax.experimental.layout import Layout, with_layout_constraint
from jax.sharding import PartitionSpec as P


GATE_ROWS = 8


def slot_targets(block_routes, experts, capacity):
    flat_routes = block_routes.reshape(-1)
    pairs = flat_routes.shape[0]
    one_hot = (flat_routes[:, None] == jnp.arange(experts, dtype=jnp.int32)[None, :]).astype(
        jnp.bfloat16
    )
    earlier = (
        jnp.arange(pairs, dtype=jnp.int32)[None, :] < jnp.arange(pairs, dtype=jnp.int32)[:, None]
    ).astype(jnp.bfloat16)
    before = jnp.dot(earlier, one_hot, preferred_element_type=jnp.float32)
    slot_rank = jnp.sum(before * one_hot.astype(jnp.float32), axis=1).astype(jnp.int32)
    return (flat_routes * capacity + slot_rank).reshape(block_routes.shape)


def silu_parts(preact):
    sigma = jax.nn.sigmoid(preact)
    return (preact * sigma, sigma * (1.0 + preact * (1.0 - sigma)))


def seq_swap(x):
    return lax.ppermute(x, "seq", [(0, 1), (1, 0)])


def expert_rows(block, input_rows, preact_rows, w_in_half, w_out_half):
    chunks, rows_per, model_width = block.shape
    capacity = rows_per - GATE_ROWS
    count = chunks * rows_per
    rows = block.reshape(count, model_width)
    row_gates = block[:, capacity, :rows_per].reshape(count, 1).astype(jnp.float32)
    raw_grad = lax.dot_general(
        rows, w_out_half, (((1,), (1,)), ((), ())), preferred_element_type=jnp.float32
    )
    activation, slope = silu_parts(preact_rows.reshape(count, -1).astype(jnp.float32))
    gate_part = jnp.sum(activation * raw_grad, axis=1)
    delta_rows = (row_gates * raw_grad * slope).astype(jnp.bfloat16)
    grad_part = lax.dot_general(
        delta_rows, w_in_half, (((1,), (1,)), ((), ())), preferred_element_type=jnp.float32
    )
    gate_rows = jnp.pad(
        gate_part.reshape(chunks, 1, rows_per),
        ((0, 0), (capacity, GATE_ROWS - 1), (0, model_width - rows_per)),
    )
    back = grad_part.reshape(chunks, rows_per, model_width) + gate_rows
    weight_part = lax.dot_general(
        input_rows.reshape(count, model_width),
        delta_rows,
        (((0,), (0,)), ((), ())),
        preferred_element_type=jnp.float32,
    )
    return back, weight_part


def on_device(out_grad, routes, gates, saved_input, saved_preact, w_in, w_out):
    model_width = out_grad.shape[1]
    experts = lax.axis_size("expert")
    halves = lax.axis_size("seq")
    data_groups = lax.axis_size("dp")
    capacity = saved_input.shape[4]
    expert_pos = lax.axis_index("expert")
    seq_pos = lax.axis_index("seq")
    rel_routes = jnp.bitwise_xor(routes, expert_pos)
    rows_per = capacity + GATE_ROWS
    cell_ids = jnp.arange(experts * rows_per, dtype=jnp.int32)
    targets = slot_targets(rel_routes, experts, capacity)
    targets = targets + (targets // capacity) * GATE_ROWS
    first_pick = targets[:, 0][None, :] == cell_ids[:, None]
    second = targets[:, 1][None, :] == cell_ids[:, None]
    send_matrix = (first_pick | second).astype(jnp.bfloat16)
    send_rows = jnp.dot(send_matrix, out_grad, preferred_element_type=jnp.float32)
    gate_cells = jnp.sum(
        jnp.where(first_pick, gates[:, 0][None, :].astype(jnp.float32), 0.0)
        + jnp.where(second, gates[:, 1][None, :].astype(jnp.float32), 0.0),
        axis=1,
    )
    gate_rows = jnp.pad(
        gate_cells.reshape(experts, 1, rows_per),
        ((0, 0), (capacity, GATE_ROWS - 1), (0, model_width - rows_per)),
    )
    payload = (send_rows.reshape(experts, rows_per, model_width) + gate_rows).astype(jnp.bfloat16)

    def pairs(ds, k):
        return [
            (ss * experts + jj, (ss ^ ds) * experts + (jj ^ k))
            for ss in range(halves)
            for jj in range(experts)
        ]

    received = {}
    for ds in range(halves):
        for k in range(experts):
            if ds == 0 and k == 0:
                received[(ds, k)] = payload[0]
            else:
                received[(ds, k)] = lax.ppermute(payload[k], ("seq", "expert"), pairs(ds, k))
    by_offset = jnp.stack(
        [jnp.stack([received[(ds, k)] for k in range(experts)]) for ds in range(halves)]
    )
    order = jnp.bitwise_xor(expert_pos, jnp.arange(experts, dtype=jnp.int32))
    seq_order = jnp.bitwise_xor(seq_pos, jnp.arange(halves, dtype=jnp.int32))
    padding = ((0, 0), (0, 0), (0, GATE_ROWS), (0, 0))
    inputs = jnp.pad(saved_input[0, 0][order[None, :], seq_order[:, None]], padding)
    preacts = jnp.pad(saved_preact[0, 0][order[None, :], seq_order[:, None]], padding)
    all_back, weight_part = expert_rows(
        by_offset.reshape(experts * halves, rows_per, model_width),
        inputs.reshape(experts * halves, rows_per, model_width),
        preacts.reshape(experts * halves, rows_per, -1),
        w_in[0],
        w_out[0],
    )
    weight_part = (weight_part * (1.0 / data_groups)).astype(jnp.bfloat16)
    weight_part = with_layout_constraint(weight_part, Layout(major_to_minor=(0, 1)))
    weight_blocks = lax.all_to_all(weight_part, "dp", split_axis=0, concat_axis=0, tiled=True)
    weight_blocks = weight_blocks.reshape(data_groups, -1, weight_blocks.shape[1])
    weight_grad = jnp.sum(weight_blocks.astype(jnp.float32), axis=0)[None]
    all_back = all_back.reshape(halves, experts, rows_per, model_width)
    partner_part = seq_swap(all_back[1].astype(jnp.bfloat16))
    summed = (all_back[0] + partner_part.astype(jnp.float32)).astype(jnp.bfloat16)
    back = [summed[0]] + [
        lax.ppermute(summed[k], "expert", [(jj, jj ^ k) for jj in range(experts)])
        for k in range(1, experts)
    ]
    back_rows = jnp.stack(back)
    back_flat = back_rows.reshape(experts * rows_per, model_width)
    input_grad = lax.dot_general(
        send_matrix, back_flat, (((0,), (0,)), ((), ())), preferred_element_type=jnp.float32
    ).astype(jnp.bfloat16)
    gate_values = back_rows[:, capacity, :rows_per].reshape(experts * rows_per).astype(jnp.float32)
    gate_first = jnp.sum(jnp.where(first_pick, gate_values[:, None], 0.0), axis=0)
    gate_second = jnp.sum(jnp.where(second, gate_values[:, None], 0.0), axis=0)
    gate_grad = jnp.stack([gate_first, gate_second], axis=1).astype(jnp.bfloat16)
    return (input_grad, gate_grad, weight_grad)


def solution(mesh):
    return jax.shard_map(
        on_device,
        mesh=mesh,
        in_specs=(
            P(("dp", "seq", "expert"), None),
            P(("dp", "seq", "expert"), None),
            P(("dp", "seq", "expert"), None),
            P("dp", "expert", None, None, None, None),
            P("dp", "expert", None, None, None, "seq"),
            P("expert", None, "seq"),
            P("expert", "seq", None),
        ),
        out_specs=(
            P(("dp", "seq", "expert"), None),
            P(("dp", "seq", "expert"), None),
            P("expert", "dp", "seq"),
        ),
        check_vma=False,
    )
```

```python
import jax
import jax.numpy as jnp
from jax import lax
from jax.sharding import PartitionSpec as P


GATE_ROWS = 8


def slot_targets(block_routes, experts, capacity):
    flat_routes = block_routes.reshape(-1)
    pairs = flat_routes.shape[0]
    one_hot = (flat_routes[:, None] == jnp.arange(experts, dtype=jnp.int32)[None, :]).astype(
        jnp.bfloat16
    )
    earlier = (
        jnp.arange(pairs, dtype=jnp.int32)[None, :] < jnp.arange(pairs, dtype=jnp.int32)[:, None]
    ).astype(jnp.bfloat16)
    before = jnp.dot(earlier, one_hot, preferred_element_type=jnp.float32)
    slot_rank = jnp.sum(before * one_hot.astype(jnp.float32), axis=1).astype(jnp.int32)
    return (flat_routes * capacity + slot_rank).reshape(block_routes.shape)


def silu_parts(preact):
    sigma = jax.nn.sigmoid(preact)
    return (preact * sigma, sigma * (1.0 + preact * (1.0 - sigma)))


def seq_swap(x):
    return lax.ppermute(x, "seq", [(0, 1), (1, 0)])


def expert_rows(block, input_rows, preact_rows, w_in_half, w_out_half):
    chunks, rows_per, model_width = block.shape
    capacity = rows_per - GATE_ROWS
    count = chunks * rows_per
    rows = block.reshape(count, model_width)
    row_gates = block[:, capacity, :rows_per].reshape(count, 1).astype(jnp.float32)
    raw_grad = lax.dot_general(
        rows, w_out_half, (((1,), (1,)), ((), ())), preferred_element_type=jnp.float32
    )
    activation, slope = silu_parts(preact_rows.reshape(count, -1).astype(jnp.float32))
    gate_part = jnp.sum(activation * raw_grad, axis=1)
    delta_rows = (row_gates * raw_grad * slope).astype(jnp.bfloat16)
    grad_part = lax.dot_general(
        delta_rows, w_in_half, (((1,), (1,)), ((), ())), preferred_element_type=jnp.float32
    )
    gate_rows = jnp.pad(
        gate_part.reshape(chunks, 1, rows_per),
        ((0, 0), (capacity, GATE_ROWS - 1), (0, model_width - rows_per)),
    )
    back = grad_part.reshape(chunks, rows_per, model_width) + gate_rows
    weight_part = lax.dot_general(
        input_rows.reshape(count, model_width),
        delta_rows,
        (((0,), (0,)), ((), ())),
        preferred_element_type=jnp.float32,
    )
    return back, weight_part


def halving_reduce_scatter(part, axis):
    n = lax.axis_size(axis)
    if n & (n - 1):
        blocks = lax.all_to_all(part.astype(jnp.bfloat16), axis, 0, 0, tiled=True)
        return jnp.sum(blocks.reshape(n, -1, part.shape[1]).astype(jnp.float32), axis=0)
    pos = lax.axis_index(axis)
    held = part.reshape(n, part.shape[0] // n, part.shape[1])
    stage = 0
    while held.shape[0] > 1:
        bit = (pos >> stage) & 1
        paired = held.reshape(held.shape[0] // 2, 2, held.shape[1], held.shape[2])
        keep = lax.dynamic_index_in_dim(paired, bit, axis=1, keepdims=False)
        send = lax.dynamic_index_in_dim(paired, 1 - bit, axis=1, keepdims=False)
        step = 1 << stage
        got = lax.ppermute(send.astype(jnp.bfloat16), axis, [(q, q ^ step) for q in range(n)])
        held = keep + got.astype(jnp.float32)
        stage += 1
    return held[0]


def on_device(out_grad, routes, gates, saved_input, saved_preact, w_in, w_out):
    model_width = out_grad.shape[1]
    experts = lax.axis_size("expert")
    halves = lax.axis_size("seq")
    data_groups = lax.axis_size("dp")
    capacity = saved_input.shape[4]
    expert_pos = lax.axis_index("expert")
    seq_pos = lax.axis_index("seq")
    rel_routes = jnp.bitwise_xor(routes, expert_pos)
    rows_per = capacity + GATE_ROWS
    cell_ids = jnp.arange(experts * rows_per, dtype=jnp.int32)
    targets = slot_targets(rel_routes, experts, capacity)
    targets = targets + (targets // capacity) * GATE_ROWS
    first_pick = targets[:, 0][None, :] == cell_ids[:, None]
    second = targets[:, 1][None, :] == cell_ids[:, None]
    send_matrix = (first_pick | second).astype(jnp.bfloat16)
    send_rows = jnp.dot(send_matrix, out_grad, preferred_element_type=jnp.float32)
    gate_cells = jnp.sum(
        jnp.where(first_pick, gates[:, 0][None, :].astype(jnp.float32), 0.0)
        + jnp.where(second, gates[:, 1][None, :].astype(jnp.float32), 0.0),
        axis=1,
    )
    gate_rows = jnp.pad(
        gate_cells.reshape(experts, 1, rows_per),
        ((0, 0), (capacity, GATE_ROWS - 1), (0, model_width - rows_per)),
    )
    payload = (send_rows.reshape(experts, rows_per, model_width) + gate_rows).astype(jnp.bfloat16)

    def pairs(ds, k):
        return [
            (ss * experts + jj, (ss ^ ds) * experts + (jj ^ k))
            for ss in range(halves)
            for jj in range(experts)
        ]

    received = {}
    for ds in range(halves):
        for k in range(experts):
            if ds == 0 and k == 0:
                received[(ds, k)] = payload[0]
            else:
                received[(ds, k)] = lax.ppermute(payload[k], ("seq", "expert"), pairs(ds, k))
    by_offset = jnp.stack(
        [jnp.stack([received[(ds, k)] for k in range(experts)]) for ds in range(halves)]
    )
    order = jnp.bitwise_xor(expert_pos, jnp.arange(experts, dtype=jnp.int32))
    seq_order = jnp.bitwise_xor(seq_pos, jnp.arange(halves, dtype=jnp.int32))
    padding = ((0, 0), (0, 0), (0, GATE_ROWS), (0, 0))
    inputs = jnp.pad(saved_input[0, 0][order[None, :], seq_order[:, None]], padding)
    preacts = jnp.pad(saved_preact[0, 0][order[None, :], seq_order[:, None]], padding)
    all_back, weight_part = expert_rows(
        by_offset.reshape(experts * halves, rows_per, model_width),
        inputs.reshape(experts * halves, rows_per, model_width),
        preacts.reshape(experts * halves, rows_per, -1),
        w_in[0],
        w_out[0],
    )
    weight_part = weight_part * (1.0 / data_groups)
    columns = weight_part.shape[1] // 2
    weight_grad = jnp.concatenate(
        [
            halving_reduce_scatter(weight_part[:, :columns], "dp"),
            halving_reduce_scatter(weight_part[:, columns:], "dp"),
        ],
        axis=1,
    )[None]
    all_back = all_back.reshape(halves, experts, rows_per, model_width)
    partner_part = seq_swap(all_back[1].astype(jnp.bfloat16))
    summed = (all_back[0] + partner_part.astype(jnp.float32)).astype(jnp.bfloat16)
    back = [summed[0]] + [
        lax.ppermute(summed[k], "expert", [(jj, jj ^ k) for jj in range(experts)])
        for k in range(1, experts)
    ]
    back_rows = jnp.stack(back)
    back_flat = back_rows.reshape(experts * rows_per, model_width)
    input_grad = lax.dot_general(
        send_matrix, back_flat, (((0,), (0,)), ((), ())), preferred_element_type=jnp.float32
    ).astype(jnp.bfloat16)
    gate_values = back_rows[:, capacity, :rows_per].reshape(experts * rows_per).astype(jnp.float32)
    gate_first = jnp.sum(jnp.where(first_pick, gate_values[:, None], 0.0), axis=0)
    gate_second = jnp.sum(jnp.where(second, gate_values[:, None], 0.0), axis=0)
    gate_grad = jnp.stack([gate_first, gate_second], axis=1).astype(jnp.bfloat16)
    return (input_grad, gate_grad, weight_grad)


def solution(mesh):
    return jax.shard_map(
        on_device,
        mesh=mesh,
        in_specs=(
            P(("dp", "seq", "expert"), None),
            P(("dp", "seq", "expert"), None),
            P(("dp", "seq", "expert"), None),
            P("dp", "expert", None, None, None, None),
            P("dp", "expert", None, None, None, "seq"),
            P("expert", None, "seq"),
            P("expert", "seq", None),
        ),
        out_specs=(
            P(("dp", "seq", "expert"), None),
            P(("dp", "seq", "expert"), None),
            P("expert", "dp", "seq"),
        ),
        check_vma=False,
    )
```

```python
import jax
import jax.numpy as jnp
from jax import lax
from jax.sharding import PartitionSpec as P


GATE_ROWS = 8


def slot_targets(block_routes, experts, capacity):
    flat_routes = block_routes.reshape(-1)
    pairs = flat_routes.shape[0]
    one_hot = (flat_routes[:, None] == jnp.arange(experts, dtype=jnp.int32)[None, :]).astype(
        jnp.bfloat16
    )
    earlier = (
        jnp.arange(pairs, dtype=jnp.int32)[None, :] < jnp.arange(pairs, dtype=jnp.int32)[:, None]
    ).astype(jnp.bfloat16)
    before = jnp.dot(earlier, one_hot, preferred_element_type=jnp.float32)
    slot_rank = jnp.sum(before * one_hot.astype(jnp.float32), axis=1).astype(jnp.int32)
    return (flat_routes * capacity + slot_rank).reshape(block_routes.shape)


def silu_parts(preact):
    sigma = jax.nn.sigmoid(preact)
    return (preact * sigma, sigma * (1.0 + preact * (1.0 - sigma)))


def seq_swap(x):
    return lax.ppermute(x, "seq", [(0, 1), (1, 0)])


def expert_rows(block, input_rows, preact_rows, w_in_half, w_out_half):
    chunks, rows_per, model_width = block.shape
    capacity = rows_per - GATE_ROWS
    count = chunks * rows_per
    rows = block.reshape(count, model_width)
    row_gates = block[:, capacity, :rows_per].reshape(count, 1).astype(jnp.float32)
    raw_grad = lax.dot_general(
        rows, w_out_half, (((1,), (1,)), ((), ())), preferred_element_type=jnp.float32
    )
    activation, slope = silu_parts(preact_rows.reshape(count, -1).astype(jnp.float32))
    gate_part = jnp.sum(activation * raw_grad, axis=1)
    delta_rows = (row_gates * raw_grad * slope).astype(jnp.bfloat16)
    grad_part = lax.dot_general(
        delta_rows, w_in_half, (((1,), (1,)), ((), ())), preferred_element_type=jnp.float32
    )
    gate_rows = jnp.pad(
        gate_part.reshape(chunks, 1, rows_per),
        ((0, 0), (capacity, GATE_ROWS - 1), (0, model_width - rows_per)),
    )
    back = grad_part.reshape(chunks, rows_per, model_width) + gate_rows
    weight_part = lax.dot_general(
        input_rows.reshape(count, model_width),
        delta_rows,
        (((0,), (0,)), ((), ())),
        preferred_element_type=jnp.float32,
    )
    return back, weight_part


def halving_reduce_scatter(part, axis):
    n = lax.axis_size(axis)
    if n & (n - 1):
        blocks = lax.all_to_all(part.astype(jnp.bfloat16), axis, 0, 0, tiled=True)
        return jnp.sum(blocks.reshape(n, -1, part.shape[1]).astype(jnp.float32), axis=0)
    pos = lax.axis_index(axis)
    held = part.reshape(n, part.shape[0] // n, part.shape[1])
    stage = 0
    while held.shape[0] > 1:
        bit = (pos >> stage) & 1
        paired = held.reshape(held.shape[0] // 2, 2, held.shape[1], held.shape[2])
        keep = lax.dynamic_index_in_dim(paired, bit, axis=1, keepdims=False)
        send = lax.dynamic_index_in_dim(paired, 1 - bit, axis=1, keepdims=False)
        step = 1 << stage
        got = lax.ppermute(send.astype(jnp.bfloat16), axis, [(q, q ^ step) for q in range(n)])
        held = keep + got.astype(jnp.float32)
        stage += 1
    return held[0]


def on_device(out_grad, routes, gates, saved_input, saved_preact, w_in, w_out):
    model_width = out_grad.shape[1]
    experts = lax.axis_size("expert")
    halves = lax.axis_size("seq")
    data_groups = lax.axis_size("dp")
    capacity = saved_input.shape[4]
    expert_pos = lax.axis_index("expert")
    seq_pos = lax.axis_index("seq")
    rel_routes = jnp.bitwise_xor(routes, expert_pos)
    rows_per = capacity + GATE_ROWS
    cell_ids = jnp.arange(experts * rows_per, dtype=jnp.int32)
    targets = slot_targets(rel_routes, experts, capacity)
    targets = targets + (targets // capacity) * GATE_ROWS
    first_pick = targets[:, 0][None, :] == cell_ids[:, None]
    second = targets[:, 1][None, :] == cell_ids[:, None]
    send_matrix = (first_pick | second).astype(jnp.bfloat16)
    send_rows = jnp.dot(send_matrix, out_grad, preferred_element_type=jnp.float32)
    gate_cells = jnp.sum(
        jnp.where(first_pick, gates[:, 0][None, :].astype(jnp.float32), 0.0)
        + jnp.where(second, gates[:, 1][None, :].astype(jnp.float32), 0.0),
        axis=1,
    )
    gate_rows = jnp.pad(
        gate_cells.reshape(experts, 1, rows_per),
        ((0, 0), (capacity, GATE_ROWS - 1), (0, model_width - rows_per)),
    )
    payload = (send_rows.reshape(experts, rows_per, model_width) + gate_rows).astype(jnp.bfloat16)

    def pairs(ds, k):
        return [
            (ss * experts + jj, (ss ^ ds) * experts + (jj ^ k))
            for ss in range(halves)
            for jj in range(experts)
        ]

    received = {}
    for ds in range(halves):
        for k in range(experts):
            if ds == 0 and k == 0:
                received[(ds, k)] = payload[0]
            else:
                received[(ds, k)] = lax.ppermute(payload[k], ("seq", "expert"), pairs(ds, k))
    by_offset = jnp.stack(
        [jnp.stack([received[(ds, k)] for k in range(experts)]) for ds in range(halves)]
    )
    order = jnp.bitwise_xor(expert_pos, jnp.arange(experts, dtype=jnp.int32))
    seq_order = jnp.bitwise_xor(seq_pos, jnp.arange(halves, dtype=jnp.int32))
    padding = ((0, 0), (0, 0), (0, GATE_ROWS), (0, 0))
    inputs = jnp.pad(saved_input[0, 0][order[None, :], seq_order[:, None]], padding)
    preacts = jnp.pad(saved_preact[0, 0][order[None, :], seq_order[:, None]], padding)
    all_back, weight_part = expert_rows(
        by_offset.reshape(experts * halves, rows_per, model_width),
        inputs.reshape(experts * halves, rows_per, model_width),
        preacts.reshape(experts * halves, rows_per, -1),
        w_in[0],
        w_out[0],
    )
    weight_part = weight_part * (1.0 / data_groups)
    pieces = 4
    columns = weight_part.shape[1] // pieces
    weight_grad = jnp.concatenate(
        [
            halving_reduce_scatter(weight_part[:, c * columns : (c + 1) * columns], "dp")
            for c in range(pieces)
        ],
        axis=1,
    )[None]
    all_back = all_back.reshape(halves, experts, rows_per, model_width)
    partner_part = seq_swap(all_back[1].astype(jnp.bfloat16))
    summed = (all_back[0] + partner_part.astype(jnp.float32)).astype(jnp.bfloat16)
    back = [summed[0]] + [
        lax.ppermute(summed[k], "expert", [(jj, jj ^ k) for jj in range(experts)])
        for k in range(1, experts)
    ]
    back_rows = jnp.stack(back)
    back_flat = back_rows.reshape(experts * rows_per, model_width)
    input_grad = lax.dot_general(
        send_matrix, back_flat, (((0,), (0,)), ((), ())), preferred_element_type=jnp.float32
    ).astype(jnp.bfloat16)
    gate_values = back_rows[:, capacity, :rows_per].reshape(experts * rows_per).astype(jnp.float32)
    gate_first = jnp.sum(jnp.where(first_pick, gate_values[:, None], 0.0), axis=0)
    gate_second = jnp.sum(jnp.where(second, gate_values[:, None], 0.0), axis=0)
    gate_grad = jnp.stack([gate_first, gate_second], axis=1).astype(jnp.bfloat16)
    return (input_grad, gate_grad, weight_grad)


def solution(mesh):
    return jax.shard_map(
        on_device,
        mesh=mesh,
        in_specs=(
            P(("dp", "seq", "expert"), None),
            P(("dp", "seq", "expert"), None),
            P(("dp", "seq", "expert"), None),
            P("dp", "expert", None, None, None, None),
            P("dp", "expert", None, None, None, "seq"),
            P("expert", None, "seq"),
            P("expert", "seq", None),
        ),
        out_specs=(
            P(("dp", "seq", "expert"), None),
            P(("dp", "seq", "expert"), None),
            P("expert", "dp", "seq"),
        ),
        check_vma=False,
    )
```

```python
import jax
import jax.numpy as jnp
from jax import lax
from jax.sharding import PartitionSpec as P


GATE_ROWS = 8


def slot_targets(block_routes, experts, capacity):
    flat_routes = block_routes.reshape(-1)
    pairs = flat_routes.shape[0]
    one_hot = (flat_routes[:, None] == jnp.arange(experts, dtype=jnp.int32)[None, :]).astype(
        jnp.bfloat16
    )
    earlier = (
        jnp.arange(pairs, dtype=jnp.int32)[None, :] < jnp.arange(pairs, dtype=jnp.int32)[:, None]
    ).astype(jnp.bfloat16)
    before = jnp.dot(earlier, one_hot, preferred_element_type=jnp.float32)
    slot_rank = jnp.sum(before * one_hot.astype(jnp.float32), axis=1).astype(jnp.int32)
    return (flat_routes * capacity + slot_rank).reshape(block_routes.shape)


def silu_parts(preact):
    sigma = jax.nn.sigmoid(preact)
    return (preact * sigma, sigma * (1.0 + preact * (1.0 - sigma)))


def seq_swap(x):
    return lax.ppermute(x, "seq", [(0, 1), (1, 0)])


def expert_rows(block, input_rows, preact_rows, w_in_half, w_out_half):
    chunks, rows_per, model_width = block.shape
    capacity = rows_per - GATE_ROWS
    count = chunks * rows_per
    rows = block.reshape(count, model_width)
    row_gates = block[:, capacity, :rows_per].reshape(count, 1).astype(jnp.float32)
    raw_grad = lax.dot_general(
        rows, w_out_half, (((1,), (1,)), ((), ())), preferred_element_type=jnp.float32
    )
    activation, slope = silu_parts(preact_rows.reshape(count, -1).astype(jnp.float32))
    gate_part = jnp.sum(activation * raw_grad, axis=1)
    delta_rows = (row_gates * raw_grad * slope).astype(jnp.bfloat16)
    grad_part = lax.dot_general(
        delta_rows, w_in_half, (((1,), (1,)), ((), ())), preferred_element_type=jnp.float32
    )
    gate_rows = jnp.pad(
        gate_part.reshape(chunks, 1, rows_per),
        ((0, 0), (capacity, GATE_ROWS - 1), (0, model_width - rows_per)),
    )
    back = grad_part.reshape(chunks, rows_per, model_width) + gate_rows
    weight_part = lax.dot_general(
        input_rows.reshape(count, model_width),
        delta_rows,
        (((0,), (0,)), ((), ())),
        preferred_element_type=jnp.float32,
    )
    return back, weight_part


def halving_reduce_scatter(parts, axis):
    n = lax.axis_size(axis)
    if n & (n - 1):
        out = []
        for part in parts:
            blocks = lax.all_to_all(part.astype(jnp.bfloat16), axis, 0, 0, tiled=True)
            out.append(jnp.sum(blocks.reshape(n, -1, part.shape[1]).astype(jnp.float32), axis=0))
        return out
    pos = lax.axis_index(axis)
    out = []
    landed = None
    for part in parts:
        held = part.reshape(n, part.shape[0] // n, part.shape[1])
        stage = 0
        while held.shape[0] > 1:
            bit = (pos >> stage) & 1
            paired = held.reshape(held.shape[0] // 2, 2, held.shape[1], held.shape[2])
            keep = lax.dynamic_index_in_dim(paired, bit, axis=1, keepdims=False)
            send = lax.dynamic_index_in_dim(paired, 1 - bit, axis=1, keepdims=False)
            if stage == 0 and landed is not None:
                send = send + landed
            step = 1 << stage
            got = lax.ppermute(send.astype(jnp.bfloat16), axis, [(q, q ^ step) for q in range(n)])
            if stage == 0:
                landed = got[0, 0, 0].astype(jnp.float32) * 0.0
            held = keep + got.astype(jnp.float32)
            stage += 1
        out.append(held[0])
    return out


def on_device(out_grad, routes, gates, saved_input, saved_preact, w_in, w_out):
    model_width = out_grad.shape[1]
    experts = lax.axis_size("expert")
    halves = lax.axis_size("seq")
    data_groups = lax.axis_size("dp")
    capacity = saved_input.shape[4]
    expert_pos = lax.axis_index("expert")
    seq_pos = lax.axis_index("seq")
    rel_routes = jnp.bitwise_xor(routes, expert_pos)
    rows_per = capacity + GATE_ROWS
    cell_ids = jnp.arange(experts * rows_per, dtype=jnp.int32)
    targets = slot_targets(rel_routes, experts, capacity)
    targets = targets + (targets // capacity) * GATE_ROWS
    first_pick = targets[:, 0][None, :] == cell_ids[:, None]
    second = targets[:, 1][None, :] == cell_ids[:, None]
    send_matrix = (first_pick | second).astype(jnp.bfloat16)
    send_rows = jnp.dot(send_matrix, out_grad, preferred_element_type=jnp.float32)
    gate_cells = jnp.sum(
        jnp.where(first_pick, gates[:, 0][None, :].astype(jnp.float32), 0.0)
        + jnp.where(second, gates[:, 1][None, :].astype(jnp.float32), 0.0),
        axis=1,
    )
    gate_rows = jnp.pad(
        gate_cells.reshape(experts, 1, rows_per),
        ((0, 0), (capacity, GATE_ROWS - 1), (0, model_width - rows_per)),
    )
    payload = (send_rows.reshape(experts, rows_per, model_width) + gate_rows).astype(jnp.bfloat16)

    def pairs(ds, k):
        return [
            (ss * experts + jj, (ss ^ ds) * experts + (jj ^ k))
            for ss in range(halves)
            for jj in range(experts)
        ]

    received = {}
    for ds in range(halves):
        for k in range(experts):
            if ds == 0 and k == 0:
                received[(ds, k)] = payload[0]
            else:
                received[(ds, k)] = lax.ppermute(payload[k], ("seq", "expert"), pairs(ds, k))
    by_offset = jnp.stack(
        [jnp.stack([received[(ds, k)] for k in range(experts)]) for ds in range(halves)]
    )
    order = jnp.bitwise_xor(expert_pos, jnp.arange(experts, dtype=jnp.int32))
    seq_order = jnp.bitwise_xor(seq_pos, jnp.arange(halves, dtype=jnp.int32))
    padding = ((0, 0), (0, 0), (0, GATE_ROWS), (0, 0))
    inputs = jnp.pad(saved_input[0, 0][order[None, :], seq_order[:, None]], padding)
    preacts = jnp.pad(saved_preact[0, 0][order[None, :], seq_order[:, None]], padding)
    all_back, weight_part = expert_rows(
        by_offset.reshape(experts * halves, rows_per, model_width),
        inputs.reshape(experts * halves, rows_per, model_width),
        preacts.reshape(experts * halves, rows_per, -1),
        w_in[0],
        w_out[0],
    )
    weight_part = weight_part * (1.0 / data_groups)
    columns = weight_part.shape[1] // 2
    weight_grad = jnp.concatenate(
        halving_reduce_scatter([weight_part[:, :columns], weight_part[:, columns:]], "dp"),
        axis=1,
    )[None]
    all_back = all_back.reshape(halves, experts, rows_per, model_width)
    partner_part = seq_swap(all_back[1].astype(jnp.bfloat16))
    summed = (all_back[0] + partner_part.astype(jnp.float32)).astype(jnp.bfloat16)
    back = [summed[0]] + [
        lax.ppermute(summed[k], "expert", [(jj, jj ^ k) for jj in range(experts)])
        for k in range(1, experts)
    ]
    back_rows = jnp.stack(back)
    back_flat = back_rows.reshape(experts * rows_per, model_width)
    input_grad = lax.dot_general(
        send_matrix, back_flat, (((0,), (0,)), ((), ())), preferred_element_type=jnp.float32
    ).astype(jnp.bfloat16)
    gate_values = back_rows[:, capacity, :rows_per].reshape(experts * rows_per).astype(jnp.float32)
    gate_first = jnp.sum(jnp.where(first_pick, gate_values[:, None], 0.0), axis=0)
    gate_second = jnp.sum(jnp.where(second, gate_values[:, None], 0.0), axis=0)
    gate_grad = jnp.stack([gate_first, gate_second], axis=1).astype(jnp.bfloat16)
    return (input_grad, gate_grad, weight_grad)


def solution(mesh):
    return jax.shard_map(
        on_device,
        mesh=mesh,
        in_specs=(
            P(("dp", "seq", "expert"), None),
            P(("dp", "seq", "expert"), None),
            P(("dp", "seq", "expert"), None),
            P("dp", "expert", None, None, None, None),
            P("dp", "expert", None, None, None, "seq"),
            P("expert", None, "seq"),
            P("expert", "seq", None),
        ),
        out_specs=(
            P(("dp", "seq", "expert"), None),
            P(("dp", "seq", "expert"), None),
            P("expert", "dp", "seq"),
        ),
        check_vma=False,
    )
```

```python
import jax
import jax.numpy as jnp
from jax import lax
from jax.sharding import PartitionSpec as P


GATE_ROWS = 8


def slot_targets(block_routes, experts, capacity):
    flat_routes = block_routes.reshape(-1)
    pairs = flat_routes.shape[0]
    one_hot = (flat_routes[:, None] == jnp.arange(experts, dtype=jnp.int32)[None, :]).astype(
        jnp.bfloat16
    )
    earlier = (
        jnp.arange(pairs, dtype=jnp.int32)[None, :] < jnp.arange(pairs, dtype=jnp.int32)[:, None]
    ).astype(jnp.bfloat16)
    before = jnp.dot(earlier, one_hot, preferred_element_type=jnp.float32)
    slot_rank = jnp.sum(before * one_hot.astype(jnp.float32), axis=1).astype(jnp.int32)
    return (flat_routes * capacity + slot_rank).reshape(block_routes.shape)


def silu_parts(preact):
    sigma = jax.nn.sigmoid(preact)
    return (preact * sigma, sigma * (1.0 + preact * (1.0 - sigma)))


def seq_swap(x):
    return lax.ppermute(x, "seq", [(0, 1), (1, 0)])


def expert_rows(block, input_rows, preact_rows, w_in_half, w_out_half):
    chunks, rows_per, model_width = block.shape
    capacity = rows_per - GATE_ROWS
    count = chunks * rows_per
    rows = block.reshape(count, model_width)
    row_gates = block[:, capacity, :rows_per].reshape(count, 1).astype(jnp.float32)
    raw_grad = lax.dot_general(
        rows, w_out_half, (((1,), (1,)), ((), ())), preferred_element_type=jnp.float32
    )
    activation, slope = silu_parts(preact_rows.reshape(count, -1).astype(jnp.float32))
    gate_part = jnp.sum(activation * raw_grad, axis=1)
    delta_rows = (row_gates * raw_grad * slope).astype(jnp.bfloat16)
    grad_part = lax.dot_general(
        delta_rows, w_in_half, (((1,), (1,)), ((), ())), preferred_element_type=jnp.float32
    )
    gate_rows = jnp.pad(
        gate_part.reshape(chunks, 1, rows_per),
        ((0, 0), (capacity, GATE_ROWS - 1), (0, model_width - rows_per)),
    )
    back = grad_part.reshape(chunks, rows_per, model_width) + gate_rows
    weight_part = lax.dot_general(
        input_rows.reshape(count, model_width),
        delta_rows,
        (((0,), (0,)), ((), ())),
        preferred_element_type=jnp.float32,
    )
    return back, weight_part


def halving_reduce_scatter(part, axis, top_first=False):
    n = lax.axis_size(axis)
    if n & (n - 1):
        blocks = lax.all_to_all(part.astype(jnp.bfloat16), axis, 0, 0, tiled=True)
        return jnp.sum(blocks.reshape(n, -1, part.shape[1]).astype(jnp.float32), axis=0)
    pos = lax.axis_index(axis)
    levels = n.bit_length() - 1
    held = part.reshape(n, part.shape[0] // n, part.shape[1])
    for stage in range(levels):
        level = levels - 1 - stage if top_first else stage
        bit = (pos >> level) & 1
        if top_first:
            paired = held.reshape(2, held.shape[0] // 2, held.shape[1], held.shape[2])
            keep = lax.dynamic_index_in_dim(paired, bit, axis=0, keepdims=False)
            send = lax.dynamic_index_in_dim(paired, 1 - bit, axis=0, keepdims=False)
        else:
            paired = held.reshape(held.shape[0] // 2, 2, held.shape[1], held.shape[2])
            keep = lax.dynamic_index_in_dim(paired, bit, axis=1, keepdims=False)
            send = lax.dynamic_index_in_dim(paired, 1 - bit, axis=1, keepdims=False)
        step = 1 << level
        got = lax.ppermute(send.astype(jnp.bfloat16), axis, [(q, q ^ step) for q in range(n)])
        held = keep + got.astype(jnp.float32)
    return held[0]


def on_device(out_grad, routes, gates, saved_input, saved_preact, w_in, w_out):
    model_width = out_grad.shape[1]
    experts = lax.axis_size("expert")
    halves = lax.axis_size("seq")
    data_groups = lax.axis_size("dp")
    capacity = saved_input.shape[4]
    expert_pos = lax.axis_index("expert")
    seq_pos = lax.axis_index("seq")
    rel_routes = jnp.bitwise_xor(routes, expert_pos)
    rows_per = capacity + GATE_ROWS
    cell_ids = jnp.arange(experts * rows_per, dtype=jnp.int32)
    targets = slot_targets(rel_routes, experts, capacity)
    targets = targets + (targets // capacity) * GATE_ROWS
    first_pick = targets[:, 0][None, :] == cell_ids[:, None]
    second = targets[:, 1][None, :] == cell_ids[:, None]
    send_matrix = (first_pick | second).astype(jnp.bfloat16)
    send_rows = jnp.dot(send_matrix, out_grad, preferred_element_type=jnp.float32)
    gate_cells = jnp.sum(
        jnp.where(first_pick, gates[:, 0][None, :].astype(jnp.float32), 0.0)
        + jnp.where(second, gates[:, 1][None, :].astype(jnp.float32), 0.0),
        axis=1,
    )
    gate_rows = jnp.pad(
        gate_cells.reshape(experts, 1, rows_per),
        ((0, 0), (capacity, GATE_ROWS - 1), (0, model_width - rows_per)),
    )
    payload = (send_rows.reshape(experts, rows_per, model_width) + gate_rows).astype(jnp.bfloat16)

    def pairs(ds, k):
        return [
            (ss * experts + jj, (ss ^ ds) * experts + (jj ^ k))
            for ss in range(halves)
            for jj in range(experts)
        ]

    received = {}
    for ds in range(halves):
        for k in range(experts):
            if ds == 0 and k == 0:
                received[(ds, k)] = payload[0]
            else:
                received[(ds, k)] = lax.ppermute(payload[k], ("seq", "expert"), pairs(ds, k))
    by_offset = jnp.stack(
        [jnp.stack([received[(ds, k)] for k in range(experts)]) for ds in range(halves)]
    )
    order = jnp.bitwise_xor(expert_pos, jnp.arange(experts, dtype=jnp.int32))
    seq_order = jnp.bitwise_xor(seq_pos, jnp.arange(halves, dtype=jnp.int32))
    padding = ((0, 0), (0, 0), (0, GATE_ROWS), (0, 0))
    inputs = jnp.pad(saved_input[0, 0][order[None, :], seq_order[:, None]], padding)
    preacts = jnp.pad(saved_preact[0, 0][order[None, :], seq_order[:, None]], padding)
    all_back, weight_part = expert_rows(
        by_offset.reshape(experts * halves, rows_per, model_width),
        inputs.reshape(experts * halves, rows_per, model_width),
        preacts.reshape(experts * halves, rows_per, -1),
        w_in[0],
        w_out[0],
    )
    weight_part = weight_part * (1.0 / data_groups)
    columns = weight_part.shape[1] // 2
    weight_grad = jnp.concatenate(
        [
            halving_reduce_scatter(weight_part[:, :columns], "dp"),
            halving_reduce_scatter(weight_part[:, columns:], "dp", top_first=True),
        ],
        axis=1,
    )[None]
    all_back = all_back.reshape(halves, experts, rows_per, model_width)
    partner_part = seq_swap(all_back[1].astype(jnp.bfloat16))
    summed = (all_back[0] + partner_part.astype(jnp.float32)).astype(jnp.bfloat16)
    back = [summed[0]] + [
        lax.ppermute(summed[k], "expert", [(jj, jj ^ k) for jj in range(experts)])
        for k in range(1, experts)
    ]
    back_rows = jnp.stack(back)
    back_flat = back_rows.reshape(experts * rows_per, model_width)
    input_grad = lax.dot_general(
        send_matrix, back_flat, (((0,), (0,)), ((), ())), preferred_element_type=jnp.float32
    ).astype(jnp.bfloat16)
    gate_values = back_rows[:, capacity, :rows_per].reshape(experts * rows_per).astype(jnp.float32)
    gate_first = jnp.sum(jnp.where(first_pick, gate_values[:, None], 0.0), axis=0)
    gate_second = jnp.sum(jnp.where(second, gate_values[:, None], 0.0), axis=0)
    gate_grad = jnp.stack([gate_first, gate_second], axis=1).astype(jnp.bfloat16)
    return (input_grad, gate_grad, weight_grad)


def solution(mesh):
    return jax.shard_map(
        on_device,
        mesh=mesh,
        in_specs=(
            P(("dp", "seq", "expert"), None),
            P(("dp", "seq", "expert"), None),
            P(("dp", "seq", "expert"), None),
            P("dp", "expert", None, None, None, None),
            P("dp", "expert", None, None, None, "seq"),
            P("expert", None, "seq"),
            P("expert", "seq", None),
        ),
        out_specs=(
            P(("dp", "seq", "expert"), None),
            P(("dp", "seq", "expert"), None),
            P("expert", "dp", "seq"),
        ),
        check_vma=False,
    )
```
